256 devices in a mesh: sub: 128 (over x, z, y), face: 2 (over core).
Axes of the slice: x: 4, y: 4, z: 8, core: 2. Of those that a mesh axis runs over, the one named last changes fastest.
Arguments:
- schur_blocks: float32 [128, 1024, 1024], P('sub', 'face'), may hold values from -1 to 4, as said below
- rigid_body_modes: float32 [128, 6, 1024], P('sub', None, 'face'), may hold values from -1 to 1
- load_cases: float32 [128, 1024, 128], P('sub', 'face'), may hold values from -60 to 60
- face_sizes: int32 [128, 4], P('sub', 'face'), may hold values from 128 to 256
- contact_mask: int32 [128, 1024], P('sub', 'face'), may hold values 0 or 1
- friction_mask: int32 [128, 1024], P('sub', 'face'), may hold values 0 or 1
- cluster_ids: int32 [128], P('sub'), may hold values from 0 to 15, as said below
- pairing: int32 [128, 2, 2, 1], P('sub', 'face'), may hold values from 0 to 0, as said below
Outputs:
- multipliers: float32 [128, 1024, 128], P('sub', 'face')
- residual: float32 [128, 1024, 128], P('sub', 'face')
The draws below stay inside these ranges and needn't reach their ends.
Inputs may be any that keep to these rules, and one draw needn't show every extreme that they name: `schur_blocks`: each block is symmetric and positive definite. `cluster_ids`: every cluster number names exactly 8 subdomains. Each device holds one subdomain, so every pairing entry is 0 (the identity matching); pairing[(i + 1) mod 128, c, 1, pairing[i, c, 0, g]] = g holds trivially.
All inputs are finite; a program needn't handle non-finite values. No bound on the sum of `contact_mask` or of `friction_mask` on one device may be relied on, other than what follows from the above.
Results may differ from the reference program's by a relative error of at most 0.00025.
Values sent between devices are 32-bit elements; how exact they have to be, the bound alone decides.
No kernel may reach another device: no remote copies, remote signals or barrier semaphores. Data moves between devices by JAX's collectives and lax.ppermute only.
A program may use at most 64 MiB of HBM per device.

```python
import jax
import jax.numpy as jnp
from jax import lax

SUB_DEV = 1
NRHS = 128
FS = 256
NF = 4
MODES = 6
ITERS = 2
DS = 1024
GROUPS = 128
SUBS = 128
CLUSTERS = 16


def rigid_draw(key):
    key_order = jax.random.fold_in(key, 11)
    key_modes = jax.random.fold_in(key, 12)
    key_coef = jax.random.fold_in(key, 13)
    scores = jax.random.randint(key_order, (SUBS,), 0, 1 << 16) * SUBS + jnp.arange(SUBS, dtype=jnp.int32)
    order = jnp.argsort(scores)
    cluster = (jnp.argsort(order) // 8).astype(jnp.int32)
    modes = jax.random.truncated_normal(key_modes, -3.0, 3.0, (SUBS, MODES, DS), jnp.float32)
    modes = modes / DS ** 0.5
    coef = jax.random.truncated_normal(key_coef, -3.0, 3.0, (CLUSTERS, MODES, NRHS), jnp.float32) * 6.0
    return (cluster, modes, coef)


def draw_cluster_ids(key, part):
    return rigid_draw(key)[0]


def draw_rigid_body_modes(key, part):
    return rigid_draw(key)[1]


def draw_load_cases(key, part):
    cluster, modes, coef = rigid_draw(key)
    key_noise = jax.random.fold_in(key, 14)
    scatter_copies = coef[cluster]
    smooth_part = jnp.einsum('smk,smr->skr', modes, scatter_copies)
    noise = jax.random.truncated_normal(key_noise, -3.0, 3.0, (SUBS, DS, NRHS), jnp.float32)
    return smooth_part + noise


def draw_schur_blocks(key, part):
    key_noise = jax.random.fold_in(key, 21)
    key_diag = jax.random.fold_in(key, 22)
    entries = jax.random.truncated_normal(key_noise, -3.0, 3.0, (SUBS, DS, DS), jnp.float32)
    scaled = entries * (0.5 / DS ** 0.5)
    symmetric = (scaled + jnp.swapaxes(scaled, 1, 2)) * 0.7071
    diagonal = jnp.exp(jax.random.uniform(key_diag, (SUBS, DS), jnp.float32, jnp.log(1.5), jnp.log(3.0)))
    return symmetric + diagonal[:, :, None] * jnp.eye(DS, dtype=jnp.float32)[None]


def draw_pairing(key, part):
    scores = jax.random.randint(key, (GROUPS, 2, SUB_DEV), 0, 1 << 16) * SUB_DEV + jnp.arange(SUB_DEV, dtype=jnp.int32)
    forward = jnp.argsort(scores, axis=-1).astype(jnp.int32)
    backward = jnp.argsort(jnp.roll(forward, 1, axis=0), axis=-1).astype(jnp.int32)
    return jnp.stack([forward, backward], axis=2)


def with_ends(values, stream_key, smallest, largest):
    longest = values.shape.index(max(values.shape))
    spots = []
    for shift in (0, 1):
        where = [jax.random.randint(jax.random.fold_in(stream_key, axis), (), 0, length) for axis, length in enumerate(values.shape)]
        where[longest] = (where[longest] + shift) % values.shape[longest]
        spots.append(tuple(where))
    return values.at[spots[0]].set(smallest).at[spots[1]].set(largest)


def setup_inputs(seed: int = 0) -> dict:
    seeds = jax.random.split(jax.random.key(seed), 9)
    return {
        "schur_blocks": draw_schur_blocks(jax.random.fold_in(seeds[8], 71), 0),
        "rigid_body_modes": draw_rigid_body_modes(jax.random.fold_in(seeds[8], 71), 0),
        "load_cases": draw_load_cases(jax.random.fold_in(seeds[8], 71), 0),
        "face_sizes": with_ends(jax.random.randint(seeds[3], (SUBS, NF), FS // 2, FS + 1), jax.random.fold_in(seeds[3], 1), FS // 2, FS).astype(jnp.int32),
        "contact_mask": with_ends((jax.random.randint(seeds[4], (SUBS, DS), 0, 3) < 1).astype(jnp.int32), jax.random.fold_in(seeds[4], 1), 0, 1),
        "friction_mask": with_ends((jax.random.randint(seeds[5], (SUBS, DS), 0, 2) < 1).astype(jnp.int32), jax.random.fold_in(seeds[5], 1), 0, 1),
        "cluster_ids": draw_cluster_ids(jax.random.fold_in(seeds[8], 71), 0),
        "pairing": draw_pairing(jax.random.fold_in(seeds[8], 71), 0),
    }


HIGH_ACCURACY = lax.Precision.HIGHEST

def partner_of(entry_values, pairing):
    groups = pairing.shape[0]
    per_group = pairing.shape[3]
    sub_ids = jnp.arange(groups * per_group, dtype=jnp.int32)
    group_ids = sub_ids // per_group
    local_ids = sub_ids % per_group
    face_ids = jnp.arange(NF, dtype=jnp.int32)
    face_half = face_ids // 2
    face_side = face_ids % 2
    shift_step = (1 - 2 * face_side).astype(jnp.int32)
    neighbour = (group_ids[:, None] + shift_step[None, :]) % groups
    chosen = pairing[group_ids[:, None], face_half[None, :], face_side[None, :], local_ids[:, None]]
    source = (neighbour * per_group + chosen).astype(jnp.int32)
    source_face = (face_ids + shift_step).astype(jnp.int32)
    return entry_values[source, source_face[None, :]]

def coarse_inverse(coarse_gram):
    lower_factor = jnp.linalg.cholesky(coarse_gram)
    eye_block = jnp.broadcast_to(jnp.eye(coarse_gram.shape[1], dtype=coarse_gram.dtype), coarse_gram.shape)
    inverse_factor = lax.linalg.triangular_solve(lower_factor, eye_block, left_side=True, lower=True)
    return jnp.einsum('bkm,bkn->bmn', inverse_factor, inverse_factor, precision=HIGH_ACCURACY)

def project(entry_values, rigid_body_modes, choice_matrix, inverse):
    subdomain_part = jnp.einsum('smk,skr->smr', rigid_body_modes, entry_values, precision=HIGH_ACCURACY)
    coarse = jnp.einsum('sb,smr->bmr', choice_matrix, subdomain_part, precision=HIGH_ACCURACY)
    weight_factors = jnp.einsum('bmn,bnr->bmr', inverse, coarse, precision=HIGH_ACCURACY)
    scatter_copies = jnp.einsum('sb,bmr->smr', choice_matrix, weight_factors, precision=HIGH_ACCURACY)
    return entry_values - jnp.einsum('smk,smr->skr', rigid_body_modes, scatter_copies, precision=HIGH_ACCURACY)

def dual_apply(entry_values, schur_blocks, pairing, signs):
    subs, width, columns = entry_values.shape
    shaped = entry_values.reshape(subs, NF, FS, columns)
    joined = signs * (shaped + partner_of(shaped, pairing))
    image = jnp.einsum('sij,sjr->sir', schur_blocks, joined.reshape(subs, width, columns), precision=HIGH_ACCURACY)
    signed = signs * image.reshape(subs, NF, FS, columns)
    return (signed + partner_of(signed, pairing)).reshape(subs, width, columns)

def reference(schur_blocks, rigid_body_modes, load_cases, face_sizes, contact_mask, friction_mask, cluster_ids, pairing):
    subs = schur_blocks.shape[0]
    positions = jnp.arange(FS, dtype=jnp.int32)
    inside = (positions[None, None, :] < face_sizes[:, :, None]).astype(jnp.float32).reshape(subs, NF * FS)
    blocked = (contact_mask * (1 - friction_mask)).astype(jnp.float32)
    free_mask = (inside * (1.0 - blocked))[:, :, None]
    choice_matrix = (cluster_ids[:, None] == jnp.arange(CLUSTERS, dtype=jnp.int32)[None, :]).astype(jnp.float32)
    local_gram = jnp.einsum('smk,snk->smn', rigid_body_modes, rigid_body_modes, precision=HIGH_ACCURACY)
    coarse_gram = jnp.einsum('sb,smn->bmn', choice_matrix, local_gram, precision=HIGH_ACCURACY)
    inverse = coarse_inverse(coarse_gram)
    signs = (1 - 2 * (jnp.arange(NF, dtype=jnp.int32) % 2)).astype(jnp.float32).reshape(1, NF, 1, 1)

    def operator(entry_values):
        projected = project(free_mask * entry_values, rigid_body_modes, choice_matrix, inverse)
        folded = dual_apply(projected, schur_blocks, pairing, signs)
        return free_mask * project(folded, rigid_body_modes, choice_matrix, inverse)
    residual = free_mask * project(free_mask * load_cases, rigid_body_modes, choice_matrix, inverse)
    direction = residual
    norm_now = jnp.sum(residual * residual, axis=(0, 1))
    multipliers = jnp.zeros_like(load_cases)
    for iteration in range(ITERS):
        image = operator(direction)
        step_size = norm_now / jnp.sum(direction * image, axis=(0, 1))
        multipliers = multipliers + step_size * direction
        residual = residual - step_size * image
        if iteration + 1 < ITERS:
            norm_next = jnp.sum(residual * residual, axis=(0, 1))
            direction = residual + norm_next / norm_now * direction
            norm_now = norm_next
    return (multipliers, residual)
```

```python
import jax
import jax.numpy as jnp
from jax import lax
from jax.sharding import PartitionSpec as P

ITERS = 2
AXES = ("sub", "face")
ROUNDS = ((0,), (1, 2), (3, 4), (5,), (6, 7))


HIGH_ACCURACY = lax.Precision.HIGHEST


def passed_along(value, axis, steps):
    count = lax.axis_size(axis)
    pairs = [(source, (source + steps) % count) for source in range(count)]
    return lax.ppermute(value, axis, pairs)


def total_over_devices(parts):
    count = lax.axis_size("sub") * lax.axis_size("face")
    flat = [jnp.ravel(part) for part in parts]
    sizes = [piece.shape[0] for piece in flat]
    packed = jnp.concatenate(flat)
    length = packed.shape[0]
    padded = -(-length // 1024) * 1024
    packed = jnp.pad(packed, (0, padded - length)).reshape(padded // 128, 128)
    if count & (count - 1) or count != 1 << 8:
        packed = lax.psum(packed, AXES)
    else:
        for field in ROUNDS:
            offsets = []
            for combo in range(1, 1 << len(field)):
                offsets.append(sum(1 << bit for i, bit in enumerate(field) if combo >> i & 1))
            acc = packed
            for offset in offsets:
                acc = acc + lax.ppermute(
                    packed, AXES, [(source, source ^ offset) for source in range(count)]
                )
            packed = acc
    packed = packed.reshape(padded)
    out = []
    start = 0
    for part, size in zip(parts, sizes):
        out.append(packed[start : start + size].reshape(part.shape))
        start += size
    return out


def small_inverse(gram):
    m = gram.shape[1]
    g = [[gram[:, i, j] for j in range(m)] for i in range(m)]
    low = [[None] * m for _ in range(m)]
    for j in range(m):
        acc = g[j][j]
        for k in range(j):
            acc = acc - low[j][k] * low[j][k]
        low[j][j] = jnp.sqrt(acc)
        for i in range(j + 1, m):
            acc = g[i][j]
            for k in range(j):
                acc = acc - low[i][k] * low[j][k]
            low[i][j] = acc / low[j][j]
    inv = [[None] * m for _ in range(m)]
    for c in range(m):
        for i in range(c, m):
            acc = jnp.ones_like(g[0][0]) if i == c else jnp.zeros_like(g[0][0])
            for k in range(c, i):
                acc = acc - low[i][k] * inv[k][c]
            inv[i][c] = acc / low[i][i]
    rows = []
    for a in range(m):
        row = []
        for b in range(m):
            acc = None
            for k in range(max(a, b), m):
                term = inv[k][a] * inv[k][b]
                acc = term if acc is None else acc + term
            row.append(acc)
        rows.append(jnp.stack(row, axis=-1))
    return jnp.stack(rows, axis=-2)


def on_device(
    schur_blocks,
    rigid_body_modes,
    load_cases,
    face_sizes,
    contact_mask,
    friction_mask,
    cluster_ids,
    pairing,
):
    sub_count, row_count, width = schur_blocks.shape
    columns = load_cases.shape[2]
    face_len = row_count // 2
    clusters = sub_count * lax.axis_size("sub") // 8
    positions = jnp.arange(face_len, dtype=jnp.int32)
    inside = (
        (positions[None, None, :] < face_sizes[:, :, None])
        .astype(jnp.float32)
        .reshape(sub_count, row_count)
    )
    blocked = (contact_mask * (1 - friction_mask)).astype(jnp.float32)
    free_mask = (inside * (1.0 - blocked))[:, :, None]
    choice_matrix = (cluster_ids[:, None] == jnp.arange(clusters, dtype=jnp.int32)[None, :]).astype(
        jnp.float32
    )
    face_sign = (1 - 2 * (jnp.arange(row_count, dtype=jnp.int32) // face_len)).astype(jnp.float32)[
        None, :, None
    ]
    pair_right = pairing[0, 0, 0]
    pair_left = pairing[0, 0, 1]

    def partial_coarse(entry_values):
        subdomain_part = jnp.einsum(
            "hxy,hyj->hxj", rigid_body_modes, entry_values, precision=HIGH_ACCURACY
        )
        return jnp.einsum("fo,flu->olu", choice_matrix, subdomain_part, precision=HIGH_ACCURACY)

    def apply_blocks(blocks, coarse):
        return jnp.einsum("bmn,bnr->bmr", blocks, coarse, precision=HIGH_ACCURACY)

    def spread(weight_factors):
        scatter_copies = jnp.einsum(
            "wc,cis->wis", choice_matrix, weight_factors, precision=HIGH_ACCURACY
        )
        return jnp.einsum(
            "fpd,fpx->fdx", rigid_body_modes, scatter_copies, precision=HIGH_ACCURACY
        )

    def pair_sum(a, b):
        return jnp.sum(a * b, axis=(0, 1))

    def partner(entry_values):
        shaped = entry_values.reshape(sub_count, 2, face_len, columns)
        from_right = passed_along(shaped[:, 1], "sub", -1)
        from_left = passed_along(shaped[:, 0], "sub", 1)
        matched = jnp.stack(
            [jnp.take(from_right, pair_right, axis=0), jnp.take(from_left, pair_left, axis=0)],
            axis=1,
        )
        return matched.reshape(entry_values.shape)

    local_gram = jnp.einsum(
        "gmk,gnk->gmn", rigid_body_modes, rigid_body_modes, precision=HIGH_ACCURACY
    )
    gram_part = jnp.einsum("gb,gmn->bmn", choice_matrix, local_gram, precision=HIGH_ACCURACY)
    masked_modes = rigid_body_modes * jnp.swapaxes(free_mask, 1, 2)
    local_masked_gram = jnp.einsum(
        "gmk,gnk->gmn", masked_modes, rigid_body_modes, precision=HIGH_ACCURACY
    )
    masked_gram_part = jnp.einsum(
        "gb,gmn->bmn", choice_matrix, local_masked_gram, precision=HIGH_ACCURACY
    )
    masked_loads = free_mask * load_cases
    coarse_gram, masked_gram, coarse_first, load_squares = total_over_devices(
        (gram_part, masked_gram_part, partial_coarse(masked_loads), pair_sum(masked_loads, masked_loads))
    )
    inverse = small_inverse(coarse_gram)

    first_weights = apply_blocks(inverse, coarse_first)
    residual = free_mask * (masked_loads - spread(first_weights))
    masked_first = apply_blocks(masked_gram, first_weights)
    norm_now = (
        load_squares
        - 2.0 * jnp.sum(first_weights * coarse_first, axis=(0, 1))
        + jnp.sum(first_weights * masked_first, axis=(0, 1))
    )
    coarse_res = coarse_first - masked_first
    direction = residual
    coarse_dir = coarse_res
    multipliers = jnp.zeros_like(load_cases)
    for iteration in range(ITERS):
        last = iteration + 1 == ITERS
        projected = direction - spread(apply_blocks(inverse, coarse_dir))
        joined = face_sign * (projected + partner(projected))
        image_rows = jnp.einsum(
            "gkc,gcr->gkr",
            schur_blocks,
            lax.all_gather(joined, "face", axis=1, tiled=True),
            precision=HIGH_ACCURACY,
        )
        curvature_part = pair_sum(joined, image_rows)
        signed = face_sign * image_rows
        folded = signed + partner(signed)
        masked_folded = free_mask * folded
        if last:
            coarse_out, curvature = total_over_devices((partial_coarse(folded), curvature_part))
        else:
            coarse_out, coarse_masked_out, curvature, res_dot, fold_squares = total_over_devices(
                (
                    partial_coarse(folded),
                    partial_coarse(masked_folded),
                    curvature_part,
                    pair_sum(residual, folded),
                    pair_sum(masked_folded, folded),
                )
            )
        weights = apply_blocks(inverse, coarse_out)
        image = free_mask * (folded - spread(weights))
        step_size = norm_now / curvature
        multipliers = multipliers + step_size * direction
        residual = residual - step_size * image
        if not last:
            masked_weights = apply_blocks(masked_gram, weights)
            res_image = res_dot - jnp.sum(weights * coarse_res, axis=(0, 1))
            image_squares = (
                fold_squares
                - 2.0 * jnp.sum(weights * coarse_masked_out, axis=(0, 1))
                + jnp.sum(weights * masked_weights, axis=(0, 1))
            )
            norm_next = norm_now - 2.0 * step_size * res_image + step_size * step_size * image_squares
            coarse_res = coarse_res - step_size * (coarse_masked_out - masked_weights)
            ratio = norm_next / norm_now
            direction = residual + ratio * direction
            coarse_dir = coarse_res + ratio * coarse_dir
            norm_now = norm_next
    return (multipliers, residual)


def solution(mesh):
    placed = (
        P("sub", "face", None),
        P("sub", None, "face"),
        P("sub", "face", None),
        P("sub", "face"),
        P("sub", "face"),
        P("sub", "face"),
        P("sub"),
        P("sub", "face", None, None),
    )
    return jax.shard_map(
        on_device,
        mesh=mesh,
        in_specs=placed,
        out_specs=(P("sub", "face", None), P("sub", "face", None)),
        check_vma=False,
    )
```

```python
import jax
import jax.numpy as jnp
from jax import lax
from jax.sharding import PartitionSpec as P

ITERS = 2
AXES = ("sub", "face")
ROUNDS = ((0,), (1, 2), (3, 4), (5,), (6, 7))


HIGH_ACCURACY = lax.Precision.HIGHEST


def passed_along(value, axis, steps):
    count = lax.axis_size(axis)
    pairs = [(source, (source + steps) % count) for source in range(count)]
    return lax.ppermute(value, axis, pairs)


def total_over_devices(parts):
    count = lax.axis_size("sub") * lax.axis_size("face")
    flat = [jnp.ravel(part) for part in parts]
    sizes = [piece.shape[0] for piece in flat]
    packed = jnp.concatenate(flat)
    length = packed.shape[0]
    padded = -(-length // 1024) * 1024
    packed = jnp.pad(packed, (0, padded - length)).reshape(padded // 128, 128)
    if count & (count - 1) or count != 1 << 8:
        packed = lax.psum(packed, AXES)
    else:
        for field in ROUNDS:
            offsets = []
            for combo in range(1, 1 << len(field)):
                offsets.append(sum(1 << bit for i, bit in enumerate(field) if combo >> i & 1))
            acc = packed
            for offset in offsets:
                acc = acc + lax.ppermute(
                    packed, AXES, [(source, source ^ offset) for source in range(count)]
                )
            packed = acc
    packed = packed.reshape(padded)
    out = []
    start = 0
    for part, size in zip(parts, sizes):
        out.append(packed[start : start + size].reshape(part.shape))
        start += size
    return out


def small_inverse(gram):
    m = gram.shape[1]
    g = [[gram[:, i, j] for j in range(m)] for i in range(m)]
    low = [[None] * m for _ in range(m)]
    for j in range(m):
        acc = g[j][j]
        for k in range(j):
            acc = acc - low[j][k] * low[j][k]
        low[j][j] = jnp.sqrt(acc)
        for i in range(j + 1, m):
            acc = g[i][j]
            for k in range(j):
                acc = acc - low[i][k] * low[j][k]
            low[i][j] = acc / low[j][j]
    inv = [[None] * m for _ in range(m)]
    for c in range(m):
        for i in range(c, m):
            acc = jnp.ones_like(g[0][0]) if i == c else jnp.zeros_like(g[0][0])
            for k in range(c, i):
                acc = acc - low[i][k] * inv[k][c]
            inv[i][c] = acc / low[i][i]
    rows = []
    for a in range(m):
        row = []
        for b in range(m):
            acc = None
            for k in range(max(a, b), m):
                term = inv[k][a] * inv[k][b]
                acc = term if acc is None else acc + term
            row.append(acc)
        rows.append(jnp.stack(row, axis=-1))
    return jnp.stack(rows, axis=-2)


def on_device(
    schur_blocks,
    rigid_body_modes,
    load_cases,
    face_sizes,
    contact_mask,
    friction_mask,
    cluster_ids,
    pairing,
):
    sub_count, row_count, width = schur_blocks.shape
    columns = load_cases.shape[2]
    face_len = row_count // 2
    clusters = sub_count * lax.axis_size("sub") // 8
    positions = jnp.arange(face_len, dtype=jnp.int32)
    inside = (
        (positions[None, None, :] < face_sizes[:, :, None])
        .astype(jnp.float32)
        .reshape(sub_count, row_count)
    )
    blocked = (contact_mask * (1 - friction_mask)).astype(jnp.float32)
    free_mask = (inside * (1.0 - blocked))[:, :, None]
    choice_matrix = (cluster_ids[:, None] == jnp.arange(clusters, dtype=jnp.int32)[None, :]).astype(
        jnp.float32
    )
    face_sign = (1 - 2 * (jnp.arange(row_count, dtype=jnp.int32) // face_len)).astype(jnp.float32)[
        None, :, None
    ]
    pair_right = pairing[0, 0, 0]
    pair_left = pairing[0, 0, 1]

    def partial_coarse(entry_values):
        subdomain_part = jnp.einsum(
            "hxy,hyj->hxj", rigid_body_modes, entry_values, precision=HIGH_ACCURACY
        )
        return jnp.einsum("fo,flu->olu", choice_matrix, subdomain_part, precision=HIGH_ACCURACY)

    def partial_coarse_with(modes, choice, entry_values):
        subdomain_part = jnp.einsum("hxy,hyj->hxj", modes, entry_values, precision=HIGH_ACCURACY)
        return jnp.einsum("fo,flu->olu", choice, subdomain_part, precision=HIGH_ACCURACY)

    def apply_blocks(blocks, coarse):
        return jnp.einsum("bmn,bnr->bmr", blocks, coarse, precision=HIGH_ACCURACY)

    def spread(weight_factors):
        scatter_copies = jnp.einsum(
            "wc,cis->wis", choice_matrix, weight_factors, precision=HIGH_ACCURACY
        )
        return jnp.einsum(
            "fpd,fpx->fdx", rigid_body_modes, scatter_copies, precision=HIGH_ACCURACY
        )

    def pair_sum(a, b):
        return jnp.sum(a * b, axis=(0, 1))

    def partner(entry_values):
        shaped = entry_values.reshape(sub_count, 2, face_len, entry_values.shape[-1])
        from_right = passed_along(shaped[:, 1], "sub", -1)
        from_left = passed_along(shaped[:, 0], "sub", 1)
        matched = jnp.stack(
            [jnp.take(from_right, pair_right, axis=0), jnp.take(from_left, pair_left, axis=0)],
            axis=1,
        )
        return matched.reshape(entry_values.shape)

    local_gram = jnp.einsum(
        "gmk,gnk->gmn", rigid_body_modes, rigid_body_modes, precision=HIGH_ACCURACY
    )
    gram_part = jnp.einsum("gb,gmn->bmn", choice_matrix, local_gram, precision=HIGH_ACCURACY)
    masked_modes = rigid_body_modes * jnp.swapaxes(free_mask, 1, 2)
    local_masked_gram = jnp.einsum(
        "gmk,gnk->gmn", masked_modes, rigid_body_modes, precision=HIGH_ACCURACY
    )
    masked_gram_part = jnp.einsum(
        "gb,gmn->bmn", choice_matrix, local_masked_gram, precision=HIGH_ACCURACY
    )
    modes_count = rigid_body_modes.shape[1]
    site_data = jnp.concatenate(
        [
            jnp.swapaxes(rigid_body_modes, 1, 2),
            free_mask,
            jnp.broadcast_to(choice_matrix[:, None, :], (sub_count, row_count, clusters)),
        ],
        axis=2,
    )
    partner_data = partner(site_data)
    partner_modes = jnp.swapaxes(partner_data[:, :, :modes_count], 1, 2)
    partner_masked_modes = partner_modes * jnp.swapaxes(partner_data[:, :, modes_count : modes_count + 1], 1, 2)
    partner_choice = (
        partner_data[:, 0, modes_count + 1 :],
        partner_data[:, face_len, modes_count + 1 :],
    )

    def folded_coarse(signed_rows, own_modes, other_modes):
        own = partial_coarse_with(own_modes, choice_matrix, signed_rows)
        for half in range(2):
            rows = slice(half * face_len, (half + 1) * face_len)
            own = own + partial_coarse_with(
                other_modes[:, :, rows], partner_choice[half], signed_rows[:, rows]
            )
        return own

    masked_loads = free_mask * load_cases
    coarse_gram, masked_gram, coarse_first = total_over_devices(
        (gram_part, masked_gram_part, partial_coarse(masked_loads))
    )
    inverse = small_inverse(coarse_gram)

    first_weights = apply_blocks(inverse, coarse_first)
    residual = free_mask * (masked_loads - spread(first_weights))
    coarse_res = coarse_first - apply_blocks(masked_gram, first_weights)
    multipliers = jnp.zeros_like(load_cases)
    for iteration in range(ITERS):
        last = iteration + 1 == ITERS
        projected = residual - spread(apply_blocks(inverse, coarse_res))
        joined = face_sign * (projected + partner(projected))
        image_rows = jnp.einsum(
            "gkc,gcr->gkr",
            schur_blocks,
            lax.all_gather(joined, "face", axis=1, tiled=True),
            precision=HIGH_ACCURACY,
        )
        parts = [
            folded_coarse(face_sign * image_rows, rigid_body_modes, partner_modes),
            pair_sum(joined, image_rows),
            pair_sum(residual, residual),
        ]
        if iteration:
            parts.append(pair_sum(residual, image))
        if not last:
            parts.append(folded_coarse(face_sign * image_rows, masked_modes, partner_masked_modes))
        totals = total_over_devices(parts)
        signed = face_sign * image_rows
        folded_now = signed + partner(signed)
        coarse_now, curvature_now, norm_next = totals[:3]
        masked_now = totals[-1] if not last else None
        if iteration:
            cross = totals[3]
            ratio = norm_next / norm_now
            direction = residual + ratio * direction
            curvature = curvature_now + 2.0 * ratio * cross + ratio * ratio * curvature
            coarse_out = coarse_now + ratio * coarse_out
            folded = folded_now + ratio * folded
            if not last:
                coarse_masked_out = masked_now + ratio * coarse_masked_out
        else:
            direction = residual
            curvature = curvature_now
            coarse_out = coarse_now
            folded = folded_now
            if not last:
                coarse_masked_out = masked_now
        norm_now = norm_next
        weights = apply_blocks(inverse, coarse_out)
        image = free_mask * (folded - spread(weights))
        step_size = norm_now / curvature
        multipliers = multipliers + step_size * direction
        residual = residual - step_size * image
        if not last:
            coarse_res = coarse_res - step_size * (
                coarse_masked_out - apply_blocks(masked_gram, weights)
            )
    return (multipliers, residual)


def solution(mesh):
    placed = (
        P("sub", "face", None),
        P("sub", None, "face"),
        P("sub", "face", None),
        P("sub", "face"),
        P("sub", "face"),
        P("sub", "face"),
        P("sub"),
        P("sub", "face", None, None),
    )
    return jax.shard_map(
        on_device,
        mesh=mesh,
        in_specs=placed,
        out_specs=(P("sub", "face", None), P("sub", "face", None)),
        check_vma=False,
    )
```

```python
import jax
import jax.numpy as jnp
from jax import lax
from jax.sharding import PartitionSpec as P

ITERS = 2
AXES = ("sub", "face")
ROUNDS = ((0,), (1, 2), (3, 4), (5,), (6, 7))


HIGH_ACCURACY = lax.Precision.HIGHEST


def passed_along(value, axis, steps):
    count = lax.axis_size(axis)
    pairs = [(source, (source + steps) % count) for source in range(count)]
    return lax.ppermute(value, axis, pairs)


def total_over_devices(parts):
    count = lax.axis_size("sub") * lax.axis_size("face")
    flat = [jnp.ravel(part) for part in parts]
    sizes = [piece.shape[0] for piece in flat]
    packed = jnp.concatenate(flat)
    length = packed.shape[0]
    padded = -(-length // 1024) * 1024
    packed = jnp.pad(packed, (0, padded - length)).reshape(padded // 128, 128)
    if count & (count - 1) or count != 1 << 8:
        packed = lax.psum(packed, AXES)
    else:
        for field in ROUNDS:
            offsets = []
            for combo in range(1, 1 << len(field)):
                offsets.append(sum(1 << bit for i, bit in enumerate(field) if combo >> i & 1))
            acc = packed
            for offset in offsets:
                acc = acc + lax.ppermute(
                    packed, AXES, [(source, source ^ offset) for source in range(count)]
                )
            packed = acc
    packed = packed.reshape(padded)
    out = []
    start = 0
    for part, size in zip(parts, sizes):
        out.append(packed[start : start + size].reshape(part.shape))
        start += size
    return out


def small_inverse(gram):
    m = gram.shape[1]
    g = [[gram[:, i, j] for j in range(m)] for i in range(m)]
    low = [[None] * m for _ in range(m)]
    for j in range(m):
        acc = g[j][j]
        for k in range(j):
            acc = acc - low[j][k] * low[j][k]
        low[j][j] = jnp.sqrt(acc)
        for i in range(j + 1, m):
            acc = g[i][j]
            for k in range(j):
                acc = acc - low[i][k] * low[j][k]
            low[i][j] = acc / low[j][j]
    inv = [[None] * m for _ in range(m)]
    for c in range(m):
        for i in range(c, m):
            acc = jnp.ones_like(g[0][0]) if i == c else jnp.zeros_like(g[0][0])
            for k in range(c, i):
                acc = acc - low[i][k] * inv[k][c]
            inv[i][c] = acc / low[i][i]
    rows = []
    for a in range(m):
        row = []
        for b in range(m):
            acc = None
            for k in range(max(a, b), m):
                term = inv[k][a] * inv[k][b]
                acc = term if acc is None else acc + term
            row.append(acc)
        rows.append(jnp.stack(row, axis=-1))
    return jnp.stack(rows, axis=-2)


def on_device(
    schur_blocks,
    rigid_body_modes,
    load_cases,
    face_sizes,
    contact_mask,
    friction_mask,
    cluster_ids,
    pairing,
):
    sub_count, row_count, width = schur_blocks.shape
    columns = load_cases.shape[2]
    face_len = row_count // 2
    clusters = sub_count * lax.axis_size("sub") // 8
    positions = jnp.arange(face_len, dtype=jnp.int32)
    inside = (
        (positions[None, None, :] < face_sizes[:, :, None])
        .astype(jnp.float32)
        .reshape(sub_count, row_count)
    )
    blocked = (contact_mask * (1 - friction_mask)).astype(jnp.float32)
    free_mask = (inside * (1.0 - blocked))[:, :, None]
    choice_matrix = (cluster_ids[:, None] == jnp.arange(clusters, dtype=jnp.int32)[None, :]).astype(
        jnp.float32
    )
    face_sign = (1 - 2 * (jnp.arange(row_count, dtype=jnp.int32) // face_len)).astype(jnp.float32)[
        None, :, None
    ]

    def partial_coarse(entry_values):
        subdomain_part = jnp.einsum(
            "hxy,hyj->hxj", rigid_body_modes, entry_values, precision=HIGH_ACCURACY
        )
        return jnp.einsum("fo,flu->olu", choice_matrix, subdomain_part, precision=HIGH_ACCURACY)

    def partial_coarse_with(modes, choice, entry_values):
        subdomain_part = jnp.einsum("hxy,hyj->hxj", modes, entry_values, precision=HIGH_ACCURACY)
        return jnp.einsum("fo,flu->olu", choice, subdomain_part, precision=HIGH_ACCURACY)

    def apply_blocks(blocks, coarse):
        return jnp.einsum("bmn,bnr->bmr", blocks, coarse, precision=HIGH_ACCURACY)

    def spread(weight_factors):
        scatter_copies = jnp.einsum(
            "wc,cis->wis", choice_matrix, weight_factors, precision=HIGH_ACCURACY
        )
        return jnp.einsum(
            "fpd,fpx->fdx", rigid_body_modes, scatter_copies, precision=HIGH_ACCURACY
        )

    def pair_sum(a, b):
        return jnp.sum(a * b, axis=(0, 1))

    def partner(entry_values, axis=1):
        half = entry_values.shape[axis] // 2
        lower = lax.slice_in_dim(entry_values, 0, half, axis=axis)
        upper = lax.slice_in_dim(entry_values, half, 2 * half, axis=axis)
        from_right = passed_along(upper, "sub", -1)
        from_left = passed_along(lower, "sub", 1)
        return jnp.concatenate([from_right, from_left], axis=axis)

    local_gram = jnp.einsum(
        "gmk,gnk->gmn", rigid_body_modes, rigid_body_modes, precision=HIGH_ACCURACY
    )
    gram_part = jnp.einsum("gb,gmn->bmn", choice_matrix, local_gram, precision=HIGH_ACCURACY)
    masked_modes = rigid_body_modes * jnp.swapaxes(free_mask, 1, 2)
    local_masked_gram = jnp.einsum(
        "gmk,gnk->gmn", masked_modes, rigid_body_modes, precision=HIGH_ACCURACY
    )
    masked_gram_part = jnp.einsum(
        "gb,gmn->bmn", choice_matrix, local_masked_gram, precision=HIGH_ACCURACY
    )
    modes_count = rigid_body_modes.shape[1]
    site_data = jnp.concatenate(
        [
            rigid_body_modes,
            jnp.swapaxes(free_mask, 1, 2),
            jnp.broadcast_to(choice_matrix[:, :, None], (sub_count, clusters, row_count)),
        ],
        axis=1,
    )
    partner_data = partner(site_data, axis=2)
    partner_modes = partner_data[:, :modes_count]
    partner_masked_modes = partner_modes * partner_data[:, modes_count : modes_count + 1]
    partner_choice = (
        partner_data[:, modes_count + 1 :, 0],
        partner_data[:, modes_count + 1 :, face_len],
    )

    def folded_coarse(signed_rows, own_modes, other_modes):
        own = partial_coarse_with(own_modes, choice_matrix, signed_rows)
        for half in range(2):
            rows = slice(half * face_len, (half + 1) * face_len)
            own = own + partial_coarse_with(
                other_modes[:, :, rows], partner_choice[half], signed_rows[:, rows]
            )
        return own

    masked_loads = free_mask * load_cases
    coarse_gram, masked_gram, coarse_first = total_over_devices(
        (gram_part, masked_gram_part, partial_coarse(masked_loads))
    )
    inverse = small_inverse(coarse_gram)

    first_weights = apply_blocks(inverse, coarse_first)
    residual = free_mask * (masked_loads - spread(first_weights))
    coarse_res = coarse_first - apply_blocks(masked_gram, first_weights)
    multipliers = jnp.zeros_like(load_cases)
    for iteration in range(ITERS):
        last = iteration + 1 == ITERS
        projected = residual - spread(apply_blocks(inverse, coarse_res))
        joined = face_sign * (projected + partner(projected))
        image_rows = jnp.einsum(
            "gkc,gcr->gkr",
            schur_blocks,
            lax.all_gather(joined, "face", axis=1, tiled=True),
            precision=HIGH_ACCURACY,
        )
        parts = [
            folded_coarse(face_sign * image_rows, rigid_body_modes, partner_modes),
            pair_sum(joined, image_rows),
            pair_sum(residual, residual),
        ]
        if iteration:
            parts.append(pair_sum(residual, image))
        if not last:
            parts.append(folded_coarse(face_sign * image_rows, masked_modes, partner_masked_modes))
        totals = total_over_devices(parts)
        signed = face_sign * image_rows
        folded_now = signed + partner(signed)
        coarse_now, curvature_now, norm_next = totals[:3]
        masked_now = totals[-1] if not last else None
        if iteration:
            cross = totals[3]
            ratio = norm_next / norm_now
            direction = residual + ratio * direction
            curvature = curvature_now + 2.0 * ratio * cross + ratio * ratio * curvature
            coarse_out = coarse_now + ratio * coarse_out
            folded = folded_now + ratio * folded
            if not last:
                coarse_masked_out = masked_now + ratio * coarse_masked_out
        else:
            direction = residual
            curvature = curvature_now
            coarse_out = coarse_now
            folded = folded_now
            if not last:
                coarse_masked_out = masked_now
        norm_now = norm_next
        weights = apply_blocks(inverse, coarse_out)
        image = free_mask * (folded - spread(weights))
        step_size = norm_now / curvature
        multipliers = multipliers + step_size * direction
        residual = residual - step_size * image
        if not last:
            coarse_res = coarse_res - step_size * (
                coarse_masked_out - apply_blocks(masked_gram, weights)
            )
    return (multipliers, residual)


def solution(mesh):
    placed = (
        P("sub", "face", None),
        P("sub", None, "face"),
        P("sub", "face", None),
        P("sub", "face"),
        P("sub", "face"),
        P("sub", "face"),
        P("sub"),
        P("sub", "face", None, None),
    )
    return jax.shard_map(
        on_device,
        mesh=mesh,
        in_specs=placed,
        out_specs=(P("sub", "face", None), P("sub", "face", None)),
        check_vma=False,
    )
```

```python
import jax
import jax.numpy as jnp
from jax import lax
from jax.sharding import PartitionSpec as P

ITERS = 2
AXES = ("sub", "face")
ROUNDS = ((0,), (1, 2), (3, 4), (5,), (6, 7))


HIGH_ACCURACY = lax.Precision.HIGHEST


def passed_along(value, axis, steps):
    count = lax.axis_size(axis)
    pairs = [(source, (source + steps) % count) for source in range(count)]
    return lax.ppermute(value, axis, pairs)


def total_over_devices(parts):
    count = lax.axis_size("sub") * lax.axis_size("face")
    flat = [jnp.ravel(part) for part in parts]
    sizes = [piece.shape[0] for piece in flat]
    packed = jnp.concatenate(flat)
    length = packed.shape[0]
    padded = -(-length // 1024) * 1024
    packed = jnp.pad(packed, (0, padded - length)).reshape(padded // 128, 128)
    if count & (count - 1) or count != 1 << 8:
        packed = lax.psum(packed, AXES)
    else:
        for field in ROUNDS:
            offsets = []
            for combo in range(1, 1 << len(field)):
                offsets.append(sum(1 << bit for i, bit in enumerate(field) if combo >> i & 1))
            acc = packed
            for offset in offsets:
                acc = acc + lax.ppermute(
                    packed, AXES, [(source, source ^ offset) for source in range(count)]
                )
            packed = acc
    packed = packed.reshape(padded)
    out = []
    start = 0
    for part, size in zip(parts, sizes):
        out.append(packed[start : start + size].reshape(part.shape))
        start += size
    return out


def small_inverse(gram):
    m = gram.shape[1]
    g = [[gram[:, i, j] for j in range(m)] for i in range(m)]
    low = [[None] * m for _ in range(m)]
    for j in range(m):
        acc = g[j][j]
        for k in range(j):
            acc = acc - low[j][k] * low[j][k]
        low[j][j] = jnp.sqrt(acc)
        for i in range(j + 1, m):
            acc = g[i][j]
            for k in range(j):
                acc = acc - low[i][k] * low[j][k]
            low[i][j] = acc / low[j][j]
    inv = [[None] * m for _ in range(m)]
    for c in range(m):
        for i in range(c, m):
            acc = jnp.ones_like(g[0][0]) if i == c else jnp.zeros_like(g[0][0])
            for k in range(c, i):
                acc = acc - low[i][k] * inv[k][c]
            inv[i][c] = acc / low[i][i]
    rows = []
    for a in range(m):
        row = []
        for b in range(m):
            acc = None
            for k in range(max(a, b), m):
                term = inv[k][a] * inv[k][b]
                acc = term if acc is None else acc + term
            row.append(acc)
        rows.append(jnp.stack(row, axis=-1))
    return jnp.stack(rows, axis=-2)


def on_device(
    schur_blocks,
    rigid_body_modes,
    load_cases,
    face_sizes,
    contact_mask,
    friction_mask,
    cluster_ids,
    pairing,
):
    sub_count, row_count, width = schur_blocks.shape
    columns = load_cases.shape[2]
    face_len = row_count // 2
    clusters = sub_count * lax.axis_size("sub") // 8
    positions = jnp.arange(face_len, dtype=jnp.int32)
    inside = (
        (positions[None, None, :] < face_sizes[:, :, None])
        .astype(jnp.float32)
        .reshape(sub_count, row_count)
    )
    blocked = (contact_mask * (1 - friction_mask)).astype(jnp.float32)
    free_mask = (inside * (1.0 - blocked))[:, :, None]
    choice_matrix = (cluster_ids[:, None] == jnp.arange(clusters, dtype=jnp.int32)[None, :]).astype(
        jnp.float32
    )
    face_sign = (1 - 2 * (jnp.arange(row_count, dtype=jnp.int32) // face_len)).astype(jnp.float32)[
        None, :, None
    ]

    def partial_coarse(entry_values):
        subdomain_part = jnp.einsum(
            "hxy,hyj->hxj", rigid_body_modes, entry_values, precision=HIGH_ACCURACY
        )
        return jnp.einsum("fo,flu->olu", choice_matrix, subdomain_part, precision=HIGH_ACCURACY)

    def partial_coarse_with(modes, choice, entry_values):
        subdomain_part = jnp.einsum("hxy,hyj->hxj", modes, entry_values, precision=HIGH_ACCURACY)
        return jnp.einsum("fo,flu->olu", choice, subdomain_part, precision=HIGH_ACCURACY)

    def apply_blocks(blocks, coarse):
        return jnp.einsum("bmn,bnr->bmr", blocks, coarse, precision=HIGH_ACCURACY)

    def spread(weight_factors):
        scatter_copies = jnp.einsum(
            "wc,cis->wis", choice_matrix, weight_factors, precision=HIGH_ACCURACY
        )
        return jnp.einsum(
            "fpd,fpx->fdx", rigid_body_modes, scatter_copies, precision=HIGH_ACCURACY
        )

    def pair_sum(a, b):
        return jnp.sum(a * b, axis=(0, 1))

    def partner(entry_values, axis=1):
        half = entry_values.shape[axis] // 2
        lower = lax.slice_in_dim(entry_values, 0, half, axis=axis)
        upper = lax.slice_in_dim(entry_values, half, 2 * half, axis=axis)
        from_right = passed_along(upper, "sub", -1)
        from_left = passed_along(lower, "sub", 1)
        return jnp.concatenate([from_right, from_left], axis=axis)

    local_gram = jnp.einsum(
        "gmk,gnk->gmn", rigid_body_modes, rigid_body_modes, precision=HIGH_ACCURACY
    )
    gram_part = jnp.einsum("gb,gmn->bmn", choice_matrix, local_gram, precision=HIGH_ACCURACY)
    masked_modes = rigid_body_modes * jnp.swapaxes(free_mask, 1, 2)
    local_masked_gram = jnp.einsum(
        "gmk,gnk->gmn", masked_modes, rigid_body_modes, precision=HIGH_ACCURACY
    )
    masked_gram_part = jnp.einsum(
        "gb,gmn->bmn", choice_matrix, local_masked_gram, precision=HIGH_ACCURACY
    )
    modes_count = rigid_body_modes.shape[1]
    site_data = jnp.concatenate(
        [
            rigid_body_modes,
            jnp.swapaxes(free_mask, 1, 2),
            jnp.broadcast_to(choice_matrix[:, :, None], (sub_count, clusters, row_count)),
        ],
        axis=1,
    )
    partner_data = partner(site_data, axis=2)
    partner_modes = partner_data[:, :modes_count]
    partner_free = jnp.swapaxes(partner_data[:, modes_count : modes_count + 1], 1, 2)
    partner_masked_modes = partner_modes * partner_data[:, modes_count : modes_count + 1]
    partner_choice = (
        partner_data[:, modes_count + 1 :, 0],
        partner_data[:, modes_count + 1 :, face_len],
    )

    def partner_spread(weight_factors):
        halves = []
        for half in range(2):
            rows = slice(half * face_len, (half + 1) * face_len)
            scatter_copies = jnp.einsum(
                "wc,cis->wis", partner_choice[half], weight_factors, precision=HIGH_ACCURACY
            )
            halves.append(
                jnp.einsum(
                    "fpd,fpx->fdx",
                    partner_modes[:, :, rows],
                    scatter_copies,
                    precision=HIGH_ACCURACY,
                )
            )
        return jnp.concatenate(halves, axis=1)

    def folded_coarse(signed_rows, own_modes, other_modes):
        own = partial_coarse_with(own_modes, choice_matrix, signed_rows)
        for half in range(2):
            rows = slice(half * face_len, (half + 1) * face_len)
            own = own + partial_coarse_with(
                other_modes[:, :, rows], partner_choice[half], signed_rows[:, rows]
            )
        return own

    masked_loads = free_mask * load_cases
    partner_loads = partner(masked_loads)
    coarse_gram, masked_gram, coarse_first = total_over_devices(
        (gram_part, masked_gram_part, partial_coarse(masked_loads))
    )
    inverse = small_inverse(coarse_gram)

    first_weights = apply_blocks(inverse, coarse_first)
    residual = free_mask * (masked_loads - spread(first_weights))
    partner_res = partner_free * (partner_loads - partner_spread(first_weights))
    coarse_res = coarse_first - apply_blocks(masked_gram, first_weights)
    multipliers = jnp.zeros_like(load_cases)
    for iteration in range(ITERS):
        last = iteration + 1 == ITERS
        res_weights = apply_blocks(inverse, coarse_res)
        projected = residual - spread(res_weights)
        partner_proj = partner_res - partner_spread(res_weights)
        joined = face_sign * (projected + partner_proj)
        image_rows = jnp.einsum(
            "gkc,gcr->gkr",
            schur_blocks,
            lax.all_gather(joined, "face", axis=1, tiled=True),
            precision=HIGH_ACCURACY,
        )
        parts = [
            folded_coarse(face_sign * image_rows, rigid_body_modes, partner_modes),
            pair_sum(joined, image_rows),
            pair_sum(residual, residual),
        ]
        if iteration:
            parts.append(pair_sum(residual, image))
        if not last:
            parts.append(folded_coarse(face_sign * image_rows, masked_modes, partner_masked_modes))
        totals = total_over_devices(parts)
        signed = face_sign * image_rows
        folded_now = signed + partner(signed)
        coarse_now, curvature_now, norm_next = totals[:3]
        masked_now = totals[-1] if not last else None
        if iteration:
            cross = totals[3]
            ratio = norm_next / norm_now
            direction = residual + ratio * direction
            curvature = curvature_now + 2.0 * ratio * cross + ratio * ratio * curvature
            coarse_out = coarse_now + ratio * coarse_out
            folded = folded_now + ratio * folded
            if not last:
                coarse_masked_out = masked_now + ratio * coarse_masked_out
        else:
            direction = residual
            curvature = curvature_now
            coarse_out = coarse_now
            folded = folded_now
            if not last:
                coarse_masked_out = masked_now
        norm_now = norm_next
        weights = apply_blocks(inverse, coarse_out)
        image = free_mask * (folded - spread(weights))
        step_size = norm_now / curvature
        multipliers = multipliers + step_size * direction
        residual = residual - step_size * image
        if not last:
            partner_image = partner_free * (folded - partner_spread(weights))
            partner_res = partner_res - step_size * partner_image
            coarse_res = coarse_res - step_size * (
                coarse_masked_out - apply_blocks(masked_gram, weights)
            )
    return (multipliers, residual)


def solution(mesh):
    placed = (
        P("sub", "face", None),
        P("sub", None, "face"),
        P("sub", "face", None),
        P("sub", "face"),
        P("sub", "face"),
        P("sub", "face"),
        P("sub"),
        P("sub", "face", None, None),
    )
    return jax.shard_map(
        on_device,
        mesh=mesh,
        in_specs=placed,
        out_specs=(P("sub", "face", None), P("sub", "face", None)),
        check_vma=False,
    )
```

```python
import jax
import jax.numpy as jnp
from jax import lax
from jax.sharding import PartitionSpec as P

ITERS = 2
AXES = ("sub", "face")
ROUNDS = ((0,), (1, 2), (3, 4), (5,), (6, 7))


HIGH_ACCURACY = lax.Precision.HIGHEST


def passed_along(value, axis, steps):
    count = lax.axis_size(axis)
    pairs = [(source, (source + steps) % count) for source in range(count)]
    return lax.ppermute(value, axis, pairs)


def total_over_devices(parts):
    count = lax.axis_size("sub") * lax.axis_size("face")
    flat = [jnp.ravel(part) for part in parts]
    sizes = [piece.shape[0] for piece in flat]
    packed = jnp.concatenate(flat)
    length = packed.shape[0]
    padded = -(-length // 1024) * 1024
    packed = jnp.pad(packed, (0, padded - length)).reshape(padded // 128, 128)
    if count & (count - 1) or count != 1 << 8:
        packed = lax.psum(packed, AXES)
    else:
        for field in ROUNDS:
            offsets = []
            for combo in range(1, 1 << len(field)):
                offsets.append(sum(1 << bit for i, bit in enumerate(field) if combo >> i & 1))
            acc = packed
            for offset in offsets:
                acc = acc + lax.ppermute(
                    packed, AXES, [(source, source ^ offset) for source in range(count)]
                )
            packed = acc
    packed = packed.reshape(padded)
    out = []
    start = 0
    for part, size in zip(parts, sizes):
        out.append(packed[start : start + size].reshape(part.shape))
        start += size
    return out


def small_inverse(gram):
    m = gram.shape[1]
    g = [[gram[:, i, j] for j in range(m)] for i in range(m)]
    low = [[None] * m for _ in range(m)]
    for j in range(m):
        acc = g[j][j]
        for k in range(j):
            acc = acc - low[j][k] * low[j][k]
        low[j][j] = jnp.sqrt(acc)
        for i in range(j + 1, m):
            acc = g[i][j]
            for k in range(j):
                acc = acc - low[i][k] * low[j][k]
            low[i][j] = acc / low[j][j]
    inv = [[None] * m for _ in range(m)]
    for c in range(m):
        for i in range(c, m):
            acc = jnp.ones_like(g[0][0]) if i == c else jnp.zeros_like(g[0][0])
            for k in range(c, i):
                acc = acc - low[i][k] * inv[k][c]
            inv[i][c] = acc / low[i][i]
    rows = []
    for a in range(m):
        row = []
        for b in range(m):
            acc = None
            for k in range(max(a, b), m):
                term = inv[k][a] * inv[k][b]
                acc = term if acc is None else acc + term
            row.append(acc)
        rows.append(jnp.stack(row, axis=-1))
    return jnp.stack(rows, axis=-2)


def on_device(
    schur_blocks,
    rigid_body_modes,
    load_cases,
    face_sizes,
    contact_mask,
    friction_mask,
    cluster_ids,
    pairing,
):
    sub_count, row_count, width = schur_blocks.shape
    columns = load_cases.shape[2]
    face_len = row_count // 2
    clusters = sub_count * lax.axis_size("sub") // 8
    positions = jnp.arange(face_len, dtype=jnp.int32)
    inside = (
        (positions[None, None, :] < face_sizes[:, :, None])
        .astype(jnp.float32)
        .reshape(sub_count, row_count)
    )
    blocked = (contact_mask * (1 - friction_mask)).astype(jnp.float32)
    free_mask = (inside * (1.0 - blocked))[:, :, None]
    choice_matrix = (cluster_ids[:, None] == jnp.arange(clusters, dtype=jnp.int32)[None, :]).astype(
        jnp.float32
    )
    face_sign = (1 - 2 * (jnp.arange(row_count, dtype=jnp.int32) // face_len)).astype(jnp.float32)[
        None, :, None
    ]

    def to_clusters(choice, part):
        return jnp.sum(choice[:, :, None, None] * part[:, None], axis=0)

    def select_cluster(choice, coarse):
        return jnp.sum(choice[:, :, None, None] * coarse[None], axis=1)

    def partial_coarse_with(modes, choice, entry_values):
        subdomain_part = jnp.einsum("hxy,hyj->hxj", modes, entry_values, precision=HIGH_ACCURACY)
        return to_clusters(choice, subdomain_part)

    def partial_coarse(entry_values):
        return partial_coarse_with(rigid_body_modes, choice_matrix, entry_values)

    def apply_blocks(blocks, coarse):
        return jnp.sum(blocks[:, :, :, None] * coarse[:, None, :, :], axis=2)

    def spread_with(modes, choice, weight_factors):
        scatter_copies = select_cluster(choice, weight_factors)
        return jnp.sum(modes[:, :, :, None] * scatter_copies[:, :, None, :], axis=1)

    def spread(weight_factors):
        return spread_with(rigid_body_modes, choice_matrix, weight_factors)

    def pair_sum(a, b):
        return jnp.sum(a * b, axis=(0, 1))

    def partner(entry_values, axis=1):
        half = entry_values.shape[axis] // 2
        lower = lax.slice_in_dim(entry_values, 0, half, axis=axis)
        upper = lax.slice_in_dim(entry_values, half, 2 * half, axis=axis)
        from_right = passed_along(upper, "sub", -1)
        from_left = passed_along(lower, "sub", 1)
        return jnp.concatenate([from_right, from_left], axis=axis)

    local_gram = jnp.einsum(
        "gmk,gnk->gmn", rigid_body_modes, rigid_body_modes, precision=HIGH_ACCURACY
    )
    gram_part = to_clusters(choice_matrix, local_gram)
    masked_modes = rigid_body_modes * jnp.swapaxes(free_mask, 1, 2)
    local_masked_gram = jnp.einsum(
        "gmk,gnk->gmn", masked_modes, rigid_body_modes, precision=HIGH_ACCURACY
    )
    masked_gram_part = to_clusters(choice_matrix, local_masked_gram)
    modes_count = rigid_body_modes.shape[1]
    site_data = jnp.concatenate(
        [
            rigid_body_modes,
            jnp.swapaxes(free_mask, 1, 2),
            jnp.broadcast_to(choice_matrix[:, :, None], (sub_count, clusters, row_count)),
        ],
        axis=1,
    )
    partner_data = partner(site_data, axis=2)
    partner_modes = partner_data[:, :modes_count]
    partner_free = jnp.swapaxes(partner_data[:, modes_count : modes_count + 1], 1, 2)
    partner_masked_modes = partner_modes * partner_data[:, modes_count : modes_count + 1]
    partner_choice = (
        partner_data[:, modes_count + 1 :, 0],
        partner_data[:, modes_count + 1 :, face_len],
    )

    def partner_spread(weight_factors):
        halves = []
        for half in range(2):
            rows = slice(half * face_len, (half + 1) * face_len)
            halves.append(spread_with(partner_modes[:, :, rows], partner_choice[half], weight_factors))
        return jnp.concatenate(halves, axis=1)

    def folded_coarse(signed_rows, own_modes, other_modes):
        own = partial_coarse_with(own_modes, choice_matrix, signed_rows)
        for half in range(2):
            rows = slice(half * face_len, (half + 1) * face_len)
            own = own + partial_coarse_with(
                other_modes[:, :, rows], partner_choice[half], signed_rows[:, rows]
            )
        return own

    masked_loads = free_mask * load_cases
    partner_loads = partner(masked_loads)
    coarse_gram, masked_gram, coarse_first = total_over_devices(
        (gram_part, masked_gram_part, partial_coarse(masked_loads))
    )
    inverse = small_inverse(coarse_gram)

    first_weights = apply_blocks(inverse, coarse_first)
    residual = free_mask * (masked_loads - spread(first_weights))
    partner_res = partner_free * (partner_loads - partner_spread(first_weights))
    coarse_res = coarse_first - apply_blocks(masked_gram, first_weights)
    multipliers = jnp.zeros_like(load_cases)
    for iteration in range(ITERS):
        last = iteration + 1 == ITERS
        res_weights = apply_blocks(inverse, coarse_res)
        projected = residual - spread(res_weights)
        partner_proj = partner_res - partner_spread(res_weights)
        joined = face_sign * (projected + partner_proj)
        image_rows = jnp.einsum(
            "gkc,gcr->gkr",
            schur_blocks,
            lax.all_gather(joined, "face", axis=1, tiled=True),
            precision=HIGH_ACCURACY,
        )
        parts = [
            folded_coarse(face_sign * image_rows, rigid_body_modes, partner_modes),
            pair_sum(joined, image_rows),
            pair_sum(residual, residual),
        ]
        if iteration:
            parts.append(pair_sum(residual, image))
        if not last:
            parts.append(folded_coarse(face_sign * image_rows, masked_modes, partner_masked_modes))
        totals = total_over_devices(parts)
        signed = face_sign * image_rows
        folded_now = signed + partner(signed)
        coarse_now, curvature_now, norm_next = totals[:3]
        masked_now = totals[-1] if not last else None
        if iteration:
            cross = totals[3]
            ratio = norm_next / norm_now
            direction = residual + ratio * direction
            curvature = curvature_now + 2.0 * ratio * cross + ratio * ratio * curvature
            coarse_out = coarse_now + ratio * coarse_out
            folded = folded_now + ratio * folded
            if not last:
                coarse_masked_out = masked_now + ratio * coarse_masked_out
        else:
            direction = residual
            curvature = curvature_now
            coarse_out = coarse_now
            folded = folded_now
            if not last:
                coarse_masked_out = masked_now
        norm_now = norm_next
        weights = apply_blocks(inverse, coarse_out)
        image = free_mask * (folded - spread(weights))
        step_size = norm_now / curvature
        multipliers = multipliers + step_size * direction
        residual = residual - step_size * image
        if not last:
            partner_image = partner_free * (folded - partner_spread(weights))
            partner_res = partner_res - step_size * partner_image
            coarse_res = coarse_res - step_size * (
                coarse_masked_out - apply_blocks(masked_gram, weights)
            )
    return (multipliers, residual)


def solution(mesh):
    placed = (
        P("sub", "face", None),
        P("sub", None, "face"),
        P("sub", "face", None),
        P("sub", "face"),
        P("sub", "face"),
        P("sub", "face"),
        P("sub"),
        P("sub", "face", None, None),
    )
    return jax.shard_map(
        on_device,
        mesh=mesh,
        in_specs=placed,
        out_specs=(P("sub", "face", None), P("sub", "face", None)),
        check_vma=False,
    )
```

```python
import jax
import jax.numpy as jnp
from jax import lax
from jax.experimental.layout import Layout, with_layout_constraint
from jax.sharding import PartitionSpec as P

ITERS = 2
AXES = ("sub", "face")
ROUNDS = ((0,), (1, 2), (3, 4), (5,), (6, 7))


HIGH_ACCURACY = lax.Precision.HIGHEST


def passed_along(value, axis, steps):
    count = lax.axis_size(axis)
    pairs = [(source, (source + steps) % count) for source in range(count)]
    return lax.ppermute(value, axis, pairs)


def row_major(value):
    return with_layout_constraint(value, Layout(major_to_minor=tuple(range(value.ndim))))


def total_over_devices(parts):
    count = lax.axis_size("sub") * lax.axis_size("face")
    flat = [jnp.ravel(part) for part in parts]
    sizes = [piece.shape[0] for piece in flat]
    packed = jnp.concatenate(flat)
    length = packed.shape[0]
    padded = -(-length // 1024) * 1024
    packed = jnp.pad(packed, (0, padded - length)).reshape(padded // 128, 128)
    if count & (count - 1) or count != 1 << 8:
        packed = lax.psum(packed, AXES)
    else:
        for field in ROUNDS:
            offsets = []
            for combo in range(1, 1 << len(field)):
                offsets.append(sum(1 << bit for i, bit in enumerate(field) if combo >> i & 1))
            acc = packed
            for offset in offsets:
                acc = acc + lax.ppermute(
                    packed, AXES, [(source, source ^ offset) for source in range(count)]
                )
            packed = acc
    packed = packed.reshape(padded)
    out = []
    start = 0
    for part, size in zip(parts, sizes):
        out.append(packed[start : start + size].reshape(part.shape))
        start += size
    return out


def small_inverse(gram):
    m = gram.shape[1]
    g = [[gram[:, i, j] for j in range(m)] for i in range(m)]
    low = [[None] * m for _ in range(m)]
    for j in range(m):
        acc = g[j][j]
        for k in range(j):
            acc = acc - low[j][k] * low[j][k]
        low[j][j] = jnp.sqrt(acc)
        for i in range(j + 1, m):
            acc = g[i][j]
            for k in range(j):
                acc = acc - low[i][k] * low[j][k]
            low[i][j] = acc / low[j][j]
    inv = [[None] * m for _ in range(m)]
    for c in range(m):
        for i in range(c, m):
            acc = jnp.ones_like(g[0][0]) if i == c else jnp.zeros_like(g[0][0])
            for k in range(c, i):
                acc = acc - low[i][k] * inv[k][c]
            inv[i][c] = acc / low[i][i]
    rows = []
    for a in range(m):
        row = []
        for b in range(m):
            acc = None
            for k in range(max(a, b), m):
                term = inv[k][a] * inv[k][b]
                acc = term if acc is None else acc + term
            row.append(acc)
        rows.append(jnp.stack(row, axis=-1))
    return jnp.stack(rows, axis=-2)


def on_device(
    schur_blocks,
    rigid_body_modes,
    load_cases,
    face_sizes,
    contact_mask,
    friction_mask,
    cluster_ids,
    pairing,
):
    sub_count, row_count, width = schur_blocks.shape
    columns = load_cases.shape[2]
    face_len = row_count // 2
    clusters = sub_count * lax.axis_size("sub") // 8
    positions = jnp.arange(face_len, dtype=jnp.int32)
    inside = (
        (positions[None, None, :] < face_sizes[:, :, None])
        .astype(jnp.float32)
        .reshape(sub_count, row_count)
    )
    blocked = (contact_mask * (1 - friction_mask)).astype(jnp.float32)
    free_mask = (inside * (1.0 - blocked))[:, :, None]
    choice_matrix = (cluster_ids[:, None] == jnp.arange(clusters, dtype=jnp.int32)[None, :]).astype(
        jnp.float32
    )
    face_sign = (1 - 2 * (jnp.arange(row_count, dtype=jnp.int32) // face_len)).astype(jnp.float32)[
        None, :, None
    ]

    def to_clusters(choice, part):
        return jnp.sum(choice[:, :, None, None] * part[:, None], axis=0)

    def select_cluster(choice, coarse):
        return jnp.sum(choice[:, :, None, None] * coarse[None], axis=1)

    def partial_coarse_with(modes, choice, entry_values):
        subdomain_part = jnp.einsum("hxy,hyj->hxj", modes, entry_values, precision=HIGH_ACCURACY)
        return to_clusters(choice, subdomain_part)

    def partial_coarse(entry_values):
        return partial_coarse_with(rigid_body_modes, choice_matrix, entry_values)

    def apply_blocks(blocks, coarse):
        return jnp.sum(blocks[:, :, :, None] * coarse[:, None, :, :], axis=2)

    def spread_with(modes, choice, weight_factors):
        scatter_copies = select_cluster(choice, weight_factors)
        return jnp.sum(modes[:, :, :, None] * scatter_copies[:, :, None, :], axis=1)

    def spread(weight_factors):
        return spread_with(rigid_body_modes, choice_matrix, weight_factors)

    def pair_sum(a, b):
        return jnp.sum(a * b, axis=(0, 1))

    def partner(entry_values, axis=1):
        half = entry_values.shape[axis] // 2
        lower = lax.slice_in_dim(entry_values, 0, half, axis=axis)
        upper = lax.slice_in_dim(entry_values, half, 2 * half, axis=axis)
        from_right = passed_along(upper, "sub", -1)
        from_left = passed_along(lower, "sub", 1)
        return jnp.concatenate([from_right, from_left], axis=axis)

    local_gram = jnp.einsum(
        "gmk,gnk->gmn", rigid_body_modes, rigid_body_modes, precision=HIGH_ACCURACY
    )
    gram_part = to_clusters(choice_matrix, local_gram)
    masked_modes = rigid_body_modes * jnp.swapaxes(free_mask, 1, 2)
    local_masked_gram = jnp.einsum(
        "gmk,gnk->gmn", masked_modes, rigid_body_modes, precision=HIGH_ACCURACY
    )
    masked_gram_part = to_clusters(choice_matrix, local_masked_gram)
    modes_count = rigid_body_modes.shape[1]
    site_data = jnp.concatenate(
        [
            rigid_body_modes,
            jnp.swapaxes(free_mask, 1, 2),
            jnp.broadcast_to(choice_matrix[:, :, None], (sub_count, clusters, row_count)),
        ],
        axis=1,
    )
    partner_data = partner(site_data, axis=2)
    partner_modes = partner_data[:, :modes_count]
    partner_free = jnp.swapaxes(partner_data[:, modes_count : modes_count + 1], 1, 2)
    partner_masked_modes = partner_modes * partner_data[:, modes_count : modes_count + 1]
    partner_choice = (
        partner_data[:, modes_count + 1 :, 0],
        partner_data[:, modes_count + 1 :, face_len],
    )

    def partner_spread(weight_factors):
        halves = []
        for half in range(2):
            rows = slice(half * face_len, (half + 1) * face_len)
            halves.append(spread_with(partner_modes[:, :, rows], partner_choice[half], weight_factors))
        return jnp.concatenate(halves, axis=1)

    def folded_coarse(signed_rows, own_modes, other_modes):
        own = partial_coarse_with(own_modes, choice_matrix, signed_rows)
        for half in range(2):
            rows = slice(half * face_len, (half + 1) * face_len)
            own = own + partial_coarse_with(
                other_modes[:, :, rows], partner_choice[half], signed_rows[:, rows]
            )
        return own

    masked_loads = row_major(free_mask * load_cases)
    partner_loads = partner(masked_loads)
    coarse_gram, masked_gram, coarse_first = total_over_devices(
        (gram_part, masked_gram_part, partial_coarse(masked_loads))
    )
    inverse = small_inverse(coarse_gram)

    first_weights = apply_blocks(inverse, coarse_first)
    residual = free_mask * (masked_loads - spread(first_weights))
    partner_res = partner_free * (partner_loads - partner_spread(first_weights))
    coarse_res = coarse_first - apply_blocks(masked_gram, first_weights)
    multipliers = jnp.zeros_like(load_cases)
    for iteration in range(ITERS):
        last = iteration + 1 == ITERS
        res_weights = apply_blocks(inverse, coarse_res)
        projected = residual - spread(res_weights)
        partner_proj = partner_res - partner_spread(res_weights)
        joined = face_sign * (projected + partner_proj)
        image_rows = jnp.einsum(
            "gkc,gcr->gkr",
            schur_blocks,
            lax.all_gather(joined, "face", axis=1, tiled=True),
            precision=HIGH_ACCURACY,
        )
        parts = [
            folded_coarse(face_sign * image_rows, rigid_body_modes, partner_modes),
            pair_sum(joined, image_rows),
            pair_sum(residual, residual),
        ]
        if iteration:
            parts.append(pair_sum(residual, image))
        if not last:
            parts.append(folded_coarse(face_sign * image_rows, masked_modes, partner_masked_modes))
        totals = total_over_devices(parts)
        signed = row_major(face_sign * image_rows)
        folded_now = signed + partner(signed)
        coarse_now, curvature_now, norm_next = totals[:3]
        masked_now = totals[-1] if not last else None
        if iteration:
            cross = totals[3]
            ratio = norm_next / norm_now
            direction = residual + ratio * direction
            curvature = curvature_now + 2.0 * ratio * cross + ratio * ratio * curvature
            coarse_out = coarse_now + ratio * coarse_out
            folded = folded_now + ratio * folded
            if not last:
                coarse_masked_out = masked_now + ratio * coarse_masked_out
        else:
            direction = residual
            curvature = curvature_now
            coarse_out = coarse_now
            folded = folded_now
            if not last:
                coarse_masked_out = masked_now
        norm_now = norm_next
        weights = apply_blocks(inverse, coarse_out)
        image = row_major(free_mask * (folded - spread(weights)))
        step_size = norm_now / curvature
        multipliers = row_major(multipliers + step_size * direction)
        residual = row_major(residual - step_size * image)
        if not last:
            partner_image = partner_free * (folded - partner_spread(weights))
            partner_res = partner_res - step_size * partner_image
            coarse_res = coarse_res - step_size * (
                coarse_masked_out - apply_blocks(masked_gram, weights)
            )
    return (multipliers, residual)


def solution(mesh):
    placed = (
        P("sub", "face", None),
        P("sub", None, "face"),
        P("sub", "face", None),
        P("sub", "face"),
        P("sub", "face"),
        P("sub", "face"),
        P("sub"),
        P("sub", "face", None, None),
    )
    return jax.shard_map(
        on_device,
        mesh=mesh,
        in_specs=placed,
        out_specs=(P("sub", "face", None), P("sub", "face", None)),
        check_vma=False,
    )
```

```python
import jax
import jax.numpy as jnp
from jax import lax
from jax.experimental.layout import Layout, with_layout_constraint
from jax.sharding import PartitionSpec as P

ITERS = 2
AXES = ("sub", "face")
ROUNDS = ((0,), (1, 2), (3, 4), (5,), (6, 7))


HIGH_ACCURACY = lax.Precision.HIGHEST


def passed_along(value, axis, steps):
    count = lax.axis_size(axis)
    pairs = [(source, (source + steps) % count) for source in range(count)]
    return lax.ppermute(value, axis, pairs)


def row_major(value):
    return with_layout_constraint(value, Layout(major_to_minor=tuple(range(value.ndim))))


def total_over_devices(parts):
    count = lax.axis_size("sub") * lax.axis_size("face")
    flat = [jnp.ravel(part) for part in parts]
    sizes = [piece.shape[0] for piece in flat]
    packed = jnp.concatenate(flat)
    length = packed.shape[0]
    padded = -(-length // 2048) * 2048
    packed = jnp.pad(packed, (0, padded - length)).reshape(padded // 128, 128)
    if count & (count - 1) or count != 1 << 8 or lax.axis_size("face") != 2:
        packed = lax.psum(packed, AXES)
    else:
        half = padded // 256
        lower, upper = packed[:half], packed[half:]
        core_is_first = lax.axis_index("face") == 0
        with jax.named_scope("round0"):
            kept = jnp.where(core_is_first, lower, upper)
            given = jnp.where(core_is_first, upper, lower)
            kept = kept + lax.ppermute(given, AXES, [(source, source ^ 1) for source in range(count)])
        for number, field in enumerate(ROUNDS[1:], start=1):
            offsets = []
            for combo in range(1, 1 << len(field)):
                offsets.append(sum(1 << bit for i, bit in enumerate(field) if combo >> i & 1))
            with jax.named_scope(f"round{number}"):
                acc = kept
                for offset in offsets:
                    acc = acc + lax.ppermute(
                        kept, AXES, [(source, source ^ offset) for source in range(count)]
                    )
            kept = acc
        with jax.named_scope("gather"):
            other = lax.ppermute(kept, AXES, [(source, source ^ 1) for source in range(count)])
            packed = jnp.where(
                core_is_first,
                jnp.concatenate([kept, other]),
                jnp.concatenate([other, kept]),
            )
    packed = packed.reshape(padded)
    out = []
    start = 0
    for part, size in zip(parts, sizes):
        out.append(packed[start : start + size].reshape(part.shape))
        start += size
    return out


def small_inverse(gram):
    m = gram.shape[1]
    g = [[gram[:, i, j] for j in range(m)] for i in range(m)]
    low = [[None] * m for _ in range(m)]
    for j in range(m):
        acc = g[j][j]
        for k in range(j):
            acc = acc - low[j][k] * low[j][k]
        low[j][j] = jnp.sqrt(acc)
        for i in range(j + 1, m):
            acc = g[i][j]
            for k in range(j):
                acc = acc - low[i][k] * low[j][k]
            low[i][j] = acc / low[j][j]
    inv = [[None] * m for _ in range(m)]
    for c in range(m):
        for i in range(c, m):
            acc = jnp.ones_like(g[0][0]) if i == c else jnp.zeros_like(g[0][0])
            for k in range(c, i):
                acc = acc - low[i][k] * inv[k][c]
            inv[i][c] = acc / low[i][i]
    rows = []
    for a in range(m):
        row = []
        for b in range(m):
            acc = None
            for k in range(max(a, b), m):
                term = inv[k][a] * inv[k][b]
                acc = term if acc is None else acc + term
            row.append(acc)
        rows.append(jnp.stack(row, axis=-1))
    return jnp.stack(rows, axis=-2)


def on_device(
    schur_blocks,
    rigid_body_modes,
    load_cases,
    face_sizes,
    contact_mask,
    friction_mask,
    cluster_ids,
    pairing,
):
    sub_count, row_count, width = schur_blocks.shape
    columns = load_cases.shape[2]
    face_len = row_count // 2
    clusters = sub_count * lax.axis_size("sub") // 8
    positions = jnp.arange(face_len, dtype=jnp.int32)
    inside = (
        (positions[None, None, :] < face_sizes[:, :, None])
        .astype(jnp.float32)
        .reshape(sub_count, row_count)
    )
    blocked = (contact_mask * (1 - friction_mask)).astype(jnp.float32)
    free_mask = (inside * (1.0 - blocked))[:, :, None]
    choice_matrix = (cluster_ids[:, None] == jnp.arange(clusters, dtype=jnp.int32)[None, :]).astype(
        jnp.float32
    )
    face_sign = (1 - 2 * (jnp.arange(row_count, dtype=jnp.int32) // face_len)).astype(jnp.float32)[
        None, :, None
    ]

    def to_clusters(choice, part):
        return jnp.sum(choice[:, :, None, None] * part[:, None], axis=0)

    def select_cluster(choice, coarse):
        return jnp.sum(choice[:, :, None, None] * coarse[None], axis=1)

    def partial_coarse_with(modes, choice, entry_values):
        subdomain_part = jnp.einsum("hxy,hyj->hxj", modes, entry_values, precision=HIGH_ACCURACY)
        return to_clusters(choice, subdomain_part)

    def partial_coarse(entry_values):
        return partial_coarse_with(rigid_body_modes, choice_matrix, entry_values)

    def apply_blocks(blocks, coarse):
        return jnp.sum(blocks[:, :, :, None] * coarse[:, None, :, :], axis=2)

    def spread_with(modes, choice, weight_factors):
        scatter_copies = select_cluster(choice, weight_factors)
        return jnp.sum(modes[:, :, :, None] * scatter_copies[:, :, None, :], axis=1)

    def spread(weight_factors):
        return spread_with(rigid_body_modes, choice_matrix, weight_factors)

    def pair_sum(a, b):
        return jnp.sum(a * b, axis=(0, 1))

    def partner(entry_values, axis=1):
        half = entry_values.shape[axis] // 2
        lower = lax.slice_in_dim(entry_values, 0, half, axis=axis)
        upper = lax.slice_in_dim(entry_values, half, 2 * half, axis=axis)
        from_right = passed_along(upper, "sub", -1)
        from_left = passed_along(lower, "sub", 1)
        return jnp.concatenate([from_right, from_left], axis=axis)

    local_gram = jnp.einsum(
        "gmk,gnk->gmn", rigid_body_modes, rigid_body_modes, precision=HIGH_ACCURACY
    )
    gram_part = to_clusters(choice_matrix, local_gram)
    masked_modes = rigid_body_modes * jnp.swapaxes(free_mask, 1, 2)
    local_masked_gram = jnp.einsum(
        "gmk,gnk->gmn", masked_modes, rigid_body_modes, precision=HIGH_ACCURACY
    )
    masked_gram_part = to_clusters(choice_matrix, local_masked_gram)
    modes_count = rigid_body_modes.shape[1]
    site_data = jnp.concatenate(
        [
            rigid_body_modes,
            jnp.swapaxes(free_mask, 1, 2),
            jnp.broadcast_to(choice_matrix[:, :, None], (sub_count, clusters, row_count)),
        ],
        axis=1,
    )
    partner_data = partner(site_data, axis=2)
    partner_modes = partner_data[:, :modes_count]
    partner_free = jnp.swapaxes(partner_data[:, modes_count : modes_count + 1], 1, 2)
    partner_masked_modes = partner_modes * partner_data[:, modes_count : modes_count + 1]
    partner_choice = (
        partner_data[:, modes_count + 1 :, 0],
        partner_data[:, modes_count + 1 :, face_len],
    )

    def partner_spread(weight_factors):
        halves = []
        for half in range(2):
            rows = slice(half * face_len, (half + 1) * face_len)
            halves.append(spread_with(partner_modes[:, :, rows], partner_choice[half], weight_factors))
        return jnp.concatenate(halves, axis=1)

    def folded_coarse(signed_rows, own_modes, other_modes):
        own = partial_coarse_with(own_modes, choice_matrix, signed_rows)
        for half in range(2):
            rows = slice(half * face_len, (half + 1) * face_len)
            own = own + partial_coarse_with(
                other_modes[:, :, rows], partner_choice[half], signed_rows[:, rows]
            )
        return own

    masked_loads = row_major(free_mask * load_cases)
    partner_loads = partner(masked_loads)
    coarse_gram, masked_gram, coarse_first = total_over_devices(
        (gram_part, masked_gram_part, partial_coarse(masked_loads))
    )
    inverse = small_inverse(coarse_gram)

    first_weights = apply_blocks(inverse, coarse_first)
    residual = free_mask * (masked_loads - spread(first_weights))
    partner_res = partner_free * (partner_loads - partner_spread(first_weights))
    coarse_res = coarse_first - apply_blocks(masked_gram, first_weights)
    multipliers = jnp.zeros_like(load_cases)
    for iteration in range(ITERS):
        last = iteration + 1 == ITERS
        res_weights = apply_blocks(inverse, coarse_res)
        projected = residual - spread(res_weights)
        partner_proj = partner_res - partner_spread(res_weights)
        joined = face_sign * (projected + partner_proj)
        image_rows = jnp.einsum(
            "gkc,gcr->gkr",
            schur_blocks,
            lax.all_gather(joined, "face", axis=1, tiled=True),
            precision=HIGH_ACCURACY,
        )
        parts = [
            folded_coarse(face_sign * image_rows, rigid_body_modes, partner_modes),
            pair_sum(joined, image_rows),
            pair_sum(residual, residual),
        ]
        if iteration:
            parts.append(pair_sum(residual, image))
        if not last:
            parts.append(folded_coarse(face_sign * image_rows, masked_modes, partner_masked_modes))
        totals = total_over_devices(parts)
        signed = row_major(face_sign * image_rows)
        folded_now = signed + partner(signed)
        coarse_now, curvature_now, norm_next = totals[:3]
        masked_now = totals[-1] if not last else None
        if iteration:
            cross = totals[3]
            ratio = norm_next / norm_now
            direction = residual + ratio * direction
            curvature = curvature_now + 2.0 * ratio * cross + ratio * ratio * curvature
            coarse_out = coarse_now + ratio * coarse_out
            folded = folded_now + ratio * folded
            if not last:
                coarse_masked_out = masked_now + ratio * coarse_masked_out
        else:
            direction = residual
            curvature = curvature_now
            coarse_out = coarse_now
            folded = folded_now
            if not last:
                coarse_masked_out = masked_now
        norm_now = norm_next
        weights = apply_blocks(inverse, coarse_out)
        image = row_major(free_mask * (folded - spread(weights)))
        step_size = norm_now / curvature
        multipliers = row_major(multipliers + step_size * direction)
        residual = row_major(residual - step_size * image)
        if not last:
            partner_image = partner_free * (folded - partner_spread(weights))
            partner_res = partner_res - step_size * partner_image
            coarse_res = coarse_res - step_size * (
                coarse_masked_out - apply_blocks(masked_gram, weights)
            )
    return (multipliers, residual)


def solution(mesh):
    placed = (
        P("sub", "face", None),
        P("sub", None, "face"),
        P("sub", "face", None),
        P("sub", "face"),
        P("sub", "face"),
        P("sub", "face"),
        P("sub"),
        P("sub", "face", None, None),
    )
    return jax.shard_map(
        on_device,
        mesh=mesh,
        in_specs=placed,
        out_specs=(P("sub", "face", None), P("sub", "face", None)),
        check_vma=False,
    )
```

```python
import jax
import jax.numpy as jnp
from jax import lax
from jax.experimental.layout import Layout, with_layout_constraint
from jax.sharding import PartitionSpec as P

ITERS = 2
AXES = ("sub", "face")
ROUNDS = ((0,), (1, 2), (3, 4), (5,), (6, 7))


HIGH_ACCURACY = lax.Precision.HIGHEST


def passed_along(value, axis, steps):
    count = lax.axis_size(axis)
    pairs = [(source, (source + steps) % count) for source in range(count)]
    return lax.ppermute(value, axis, pairs)


def row_major(value):
    return with_layout_constraint(value, Layout(major_to_minor=tuple(range(value.ndim))))


def total_over_devices(parts):
    count = lax.axis_size("sub") * lax.axis_size("face")
    flat = [jnp.ravel(part) for part in parts]
    sizes = [piece.shape[0] for piece in flat]
    packed = jnp.concatenate(flat)
    length = packed.shape[0]
    padded = -(-length // 2048) * 2048
    packed = jnp.pad(packed, (0, padded - length)).reshape(padded // 128, 128)
    if count & (count - 1) or count != 1 << 8 or lax.axis_size("face") != 2:
        packed = lax.psum(packed, AXES)
    else:
        half = padded // 256
        core = lax.axis_index("face")
        with jax.named_scope("round0"):
            kept = lax.dynamic_slice_in_dim(packed, core * half, half)
            given = lax.dynamic_slice_in_dim(packed, (1 - core) * half, half)
            kept = kept + lax.ppermute(given, AXES, [(source, source ^ 1) for source in range(count)])
        for number, field in enumerate(ROUNDS[1:], start=1):
            offsets = []
            for combo in range(1, 1 << len(field)):
                offsets.append(sum(1 << bit for i, bit in enumerate(field) if combo >> i & 1))
            with jax.named_scope(f"round{number}"):
                acc = kept
                for offset in offsets:
                    acc = acc + lax.ppermute(
                        kept, AXES, [(source, source ^ offset) for source in range(count)]
                    )
            kept = acc
        with jax.named_scope("gather"):
            other = lax.ppermute(kept, AXES, [(source, source ^ 1) for source in range(count)])
            packed = lax.dynamic_update_slice_in_dim(
                lax.dynamic_update_slice_in_dim(packed, kept, core * half, 0),
                other,
                (1 - core) * half,
                0,
            )
    packed = packed.reshape(padded)
    out = []
    start = 0
    for part, size in zip(parts, sizes):
        out.append(packed[start : start + size].reshape(part.shape))
        start += size
    return out


def small_inverse(gram):
    m = gram.shape[1]
    g = [[gram[:, i, j] for j in range(m)] for i in range(m)]
    low = [[None] * m for _ in range(m)]
    for j in range(m):
        acc = g[j][j]
        for k in range(j):
            acc = acc - low[j][k] * low[j][k]
        low[j][j] = jnp.sqrt(acc)
        for i in range(j + 1, m):
            acc = g[i][j]
            for k in range(j):
                acc = acc - low[i][k] * low[j][k]
            low[i][j] = acc / low[j][j]
    inv = [[None] * m for _ in range(m)]
    for c in range(m):
        for i in range(c, m):
            acc = jnp.ones_like(g[0][0]) if i == c else jnp.zeros_like(g[0][0])
            for k in range(c, i):
                acc = acc - low[i][k] * inv[k][c]
            inv[i][c] = acc / low[i][i]
    rows = []
    for a in range(m):
        row = []
        for b in range(m):
            acc = None
            for k in range(max(a, b), m):
                term = inv[k][a] * inv[k][b]
                acc = term if acc is None else acc + term
            row.append(acc)
        rows.append(jnp.stack(row, axis=-1))
    return jnp.stack(rows, axis=-2)


def on_device(
    schur_blocks,
    rigid_body_modes,
    load_cases,
    face_sizes,
    contact_mask,
    friction_mask,
    cluster_ids,
    pairing,
):
    sub_count, row_count, width = schur_blocks.shape
    columns = load_cases.shape[2]
    face_len = row_count // 2
    clusters = sub_count * lax.axis_size("sub") // 8
    positions = jnp.arange(face_len, dtype=jnp.int32)
    inside = (
        (positions[None, None, :] < face_sizes[:, :, None])
        .astype(jnp.float32)
        .reshape(sub_count, row_count)
    )
    blocked = (contact_mask * (1 - friction_mask)).astype(jnp.float32)
    free_mask = (inside * (1.0 - blocked))[:, :, None]
    choice_matrix = (cluster_ids[:, None] == jnp.arange(clusters, dtype=jnp.int32)[None, :]).astype(
        jnp.float32
    )
    face_sign = (1 - 2 * (jnp.arange(row_count, dtype=jnp.int32) // face_len)).astype(jnp.float32)[
        None, :, None
    ]

    def to_clusters(choice, part):
        return jnp.sum(choice[:, :, None, None] * part[:, None], axis=0)

    def select_cluster(choice, coarse):
        return jnp.sum(choice[:, :, None, None] * coarse[None], axis=1)

    def partial_coarse_with(modes, choice, entry_values):
        subdomain_part = jnp.einsum("hxy,hyj->hxj", modes, entry_values, precision=HIGH_ACCURACY)
        return to_clusters(choice, subdomain_part)

    def partial_coarse(entry_values):
        return partial_coarse_with(rigid_body_modes, choice_matrix, entry_values)

    def apply_blocks(blocks, coarse):
        return jnp.sum(blocks[:, :, :, None] * coarse[:, None, :, :], axis=2)

    def spread_with(modes, choice, weight_factors):
        scatter_copies = select_cluster(choice, weight_factors)
        return jnp.sum(modes[:, :, :, None] * scatter_copies[:, :, None, :], axis=1)

    def spread(weight_factors):
        return spread_with(rigid_body_modes, choice_matrix, weight_factors)

    def pair_sum(a, b):
        return jnp.sum(a * b, axis=(0, 1))

    def partner(entry_values, axis=1):
        half = entry_values.shape[axis] // 2
        lower = lax.slice_in_dim(entry_values, 0, half, axis=axis)
        upper = lax.slice_in_dim(entry_values, half, 2 * half, axis=axis)
        from_right = passed_along(upper, "sub", -1)
        from_left = passed_along(lower, "sub", 1)
        return jnp.concatenate([from_right, from_left], axis=axis)

    local_gram = jnp.einsum(
        "gmk,gnk->gmn", rigid_body_modes, rigid_body_modes, precision=HIGH_ACCURACY
    )
    gram_part = to_clusters(choice_matrix, local_gram)
    masked_modes = rigid_body_modes * jnp.swapaxes(free_mask, 1, 2)
    local_masked_gram = jnp.einsum(
        "gmk,gnk->gmn", masked_modes, rigid_body_modes, precision=HIGH_ACCURACY
    )
    masked_gram_part = to_clusters(choice_matrix, local_masked_gram)
    modes_count = rigid_body_modes.shape[1]
    site_data = jnp.concatenate(
        [
            rigid_body_modes,
            jnp.swapaxes(free_mask, 1, 2),
            jnp.broadcast_to(choice_matrix[:, :, None], (sub_count, clusters, row_count)),
        ],
        axis=1,
    )
    partner_data = partner(site_data, axis=2)
    partner_modes = partner_data[:, :modes_count]
    partner_free = jnp.swapaxes(partner_data[:, modes_count : modes_count + 1], 1, 2)
    partner_masked_modes = partner_modes * partner_data[:, modes_count : modes_count + 1]
    partner_choice = (
        partner_data[:, modes_count + 1 :, 0],
        partner_data[:, modes_count + 1 :, face_len],
    )

    def partner_spread(weight_factors):
        halves = []
        for half in range(2):
            rows = slice(half * face_len, (half + 1) * face_len)
            halves.append(spread_with(partner_modes[:, :, rows], partner_choice[half], weight_factors))
        return jnp.concatenate(halves, axis=1)

    def folded_coarse(signed_rows, own_modes, other_modes):
        own = partial_coarse_with(own_modes, choice_matrix, signed_rows)
        for half in range(2):
            rows = slice(half * face_len, (half + 1) * face_len)
            own = own + partial_coarse_with(
                other_modes[:, :, rows], partner_choice[half], signed_rows[:, rows]
            )
        return own

    masked_loads = row_major(free_mask * load_cases)
    partner_loads = partner(masked_loads)
    coarse_gram, masked_gram, coarse_first = total_over_devices(
        (gram_part, masked_gram_part, partial_coarse(masked_loads))
    )
    inverse = small_inverse(coarse_gram)

    first_weights = apply_blocks(inverse, coarse_first)
    residual = free_mask * (masked_loads - spread(first_weights))
    partner_res = partner_free * (partner_loads - partner_spread(first_weights))
    coarse_res = coarse_first - apply_blocks(masked_gram, first_weights)
    multipliers = jnp.zeros_like(load_cases)
    for iteration in range(ITERS):
        last = iteration + 1 == ITERS
        res_weights = apply_blocks(inverse, coarse_res)
        projected = residual - spread(res_weights)
        partner_proj = partner_res - partner_spread(res_weights)
        joined = face_sign * (projected + partner_proj)
        image_rows = jnp.einsum(
            "gkc,gcr->gkr",
            schur_blocks,
            lax.all_gather(joined, "face", axis=1, tiled=True),
            precision=HIGH_ACCURACY,
        )
        parts = [
            folded_coarse(face_sign * image_rows, rigid_body_modes, partner_modes),
            pair_sum(joined, image_rows),
            pair_sum(residual, residual),
        ]
        if iteration:
            parts.append(pair_sum(residual, image))
        if not last:
            parts.append(folded_coarse(face_sign * image_rows, masked_modes, partner_masked_modes))
        totals = total_over_devices(parts)
        signed = row_major(face_sign * image_rows)
        folded_now = signed + partner(signed)
        coarse_now, curvature_now, norm_next = totals[:3]
        masked_now = totals[-1] if not last else None
        if iteration:
            cross = totals[3]
            ratio = norm_next / norm_now
            direction = residual + ratio * direction
            curvature = curvature_now + 2.0 * ratio * cross + ratio * ratio * curvature
            coarse_out = coarse_now + ratio * coarse_out
            folded = folded_now + ratio * folded
            if not last:
                coarse_masked_out = masked_now + ratio * coarse_masked_out
        else:
            direction = residual
            curvature = curvature_now
            coarse_out = coarse_now
            folded = folded_now
            if not last:
                coarse_masked_out = masked_now
        norm_now = norm_next
        weights = apply_blocks(inverse, coarse_out)
        image = row_major(free_mask * (folded - spread(weights)))
        step_size = norm_now / curvature
        multipliers = row_major(multipliers + step_size * direction)
        residual = row_major(residual - step_size * image)
        if not last:
            partner_image = partner_free * (folded - partner_spread(weights))
            partner_res = partner_res - step_size * partner_image
            coarse_res = coarse_res - step_size * (
                coarse_masked_out - apply_blocks(masked_gram, weights)
            )
    return (multipliers, residual)


def solution(mesh):
    placed = (
        P("sub", "face", None),
        P("sub", None, "face"),
        P("sub", "face", None),
        P("sub", "face"),
        P("sub", "face"),
        P("sub", "face"),
        P("sub"),
        P("sub", "face", None, None),
    )
    return jax.shard_map(
        on_device,
        mesh=mesh,
        in_specs=placed,
        out_specs=(P("sub", "face", None), P("sub", "face", None)),
        check_vma=False,
    )
```

```python
import jax
import jax.numpy as jnp
from jax import lax
from jax.experimental.layout import Layout, with_layout_constraint
from jax.sharding import PartitionSpec as P

ITERS = 2
AXES = ("sub", "face")
ROUNDS = ((0,), (1, 2), (3,), (4, 5), (6, 7))


HIGH_ACCURACY = lax.Precision.HIGHEST


def passed_along(value, axis, steps):
    count = lax.axis_size(axis)
    pairs = [(source, (source + steps) % count) for source in range(count)]
    return lax.ppermute(value, axis, pairs)


def row_major(value):
    return with_layout_constraint(value, Layout(major_to_minor=tuple(range(value.ndim))))


def total_over_devices(parts):
    count = lax.axis_size("sub") * lax.axis_size("face")
    flat = [jnp.ravel(part) for part in parts]
    sizes = [piece.shape[0] for piece in flat]
    packed = jnp.concatenate(flat)
    length = packed.shape[0]
    padded = -(-length // 2048) * 2048
    packed = jnp.pad(packed, (0, padded - length)).reshape(padded // 128, 128)
    if count & (count - 1) or count != 1 << 8 or lax.axis_size("face") != 2:
        packed = lax.psum(packed, AXES)
    else:
        half = padded // 256
        core = lax.axis_index("face")
        with jax.named_scope("round0"):
            kept = lax.dynamic_slice_in_dim(packed, core * half, half)
            given = lax.dynamic_slice_in_dim(packed, (1 - core) * half, half)
            kept = kept + lax.ppermute(given, AXES, [(source, source ^ 1) for source in range(count)])
        for number, field in enumerate(ROUNDS[1:], start=1):
            offsets = []
            for combo in range(1, 1 << len(field)):
                offsets.append(sum(1 << bit for i, bit in enumerate(field) if combo >> i & 1))
            with jax.named_scope(f"round{number}"):
                acc = kept
                for offset in offsets:
                    acc = acc + lax.ppermute(
                        kept, AXES, [(source, source ^ offset) for source in range(count)]
                    )
            kept = acc
        with jax.named_scope("gather"):
            other = lax.ppermute(kept, AXES, [(source, source ^ 1) for source in range(count)])
            packed = lax.dynamic_update_slice_in_dim(
                lax.dynamic_update_slice_in_dim(packed, kept, core * half, 0),
                other,
                (1 - core) * half,
                0,
            )
    packed = packed.reshape(padded)
    out = []
    start = 0
    for part, size in zip(parts, sizes):
        out.append(packed[start : start + size].reshape(part.shape))
        start += size
    return out


def small_inverse(gram):
    m = gram.shape[1]
    g = [[gram[:, i, j] for j in range(m)] for i in range(m)]
    low = [[None] * m for _ in range(m)]
    for j in range(m):
        acc = g[j][j]
        for k in range(j):
            acc = acc - low[j][k] * low[j][k]
        low[j][j] = jnp.sqrt(acc)
        for i in range(j + 1, m):
            acc = g[i][j]
            for k in range(j):
                acc = acc - low[i][k] * low[j][k]
            low[i][j] = acc / low[j][j]
    inv = [[None] * m for _ in range(m)]
    for c in range(m):
        for i in range(c, m):
            acc = jnp.ones_like(g[0][0]) if i == c else jnp.zeros_like(g[0][0])
            for k in range(c, i):
                acc = acc - low[i][k] * inv[k][c]
            inv[i][c] = acc / low[i][i]
    rows = []
    for a in range(m):
        row = []
        for b in range(m):
            acc = None
            for k in range(max(a, b), m):
                term = inv[k][a] * inv[k][b]
                acc = term if acc is None else acc + term
            row.append(acc)
        rows.append(jnp.stack(row, axis=-1))
    return jnp.stack(rows, axis=-2)


def on_device(
    schur_blocks,
    rigid_body_modes,
    load_cases,
    face_sizes,
    contact_mask,
    friction_mask,
    cluster_ids,
    pairing,
):
    sub_count, row_count, width = schur_blocks.shape
    columns = load_cases.shape[2]
    face_len = row_count // 2
    clusters = sub_count * lax.axis_size("sub") // 8
    positions = jnp.arange(face_len, dtype=jnp.int32)
    inside = (
        (positions[None, None, :] < face_sizes[:, :, None])
        .astype(jnp.float32)
        .reshape(sub_count, row_count)
    )
    blocked = (contact_mask * (1 - friction_mask)).astype(jnp.float32)
    free_mask = (inside * (1.0 - blocked))[:, :, None]
    choice_matrix = (cluster_ids[:, None] == jnp.arange(clusters, dtype=jnp.int32)[None, :]).astype(
        jnp.float32
    )
    face_sign = (1 - 2 * (jnp.arange(row_count, dtype=jnp.int32) // face_len)).astype(jnp.float32)[
        None, :, None
    ]

    def to_clusters(choice, part):
        return jnp.sum(choice[:, :, None, None] * part[:, None], axis=0)

    def select_cluster(choice, coarse):
        return jnp.sum(choice[:, :, None, None] * coarse[None], axis=1)

    def partial_coarse_with(modes, choice, entry_values):
        subdomain_part = jnp.einsum("hxy,hyj->hxj", modes, entry_values, precision=HIGH_ACCURACY)
        return to_clusters(choice, subdomain_part)

    def partial_coarse(entry_values):
        return partial_coarse_with(rigid_body_modes, choice_matrix, entry_values)

    def apply_blocks(blocks, coarse):
        return jnp.sum(blocks[:, :, :, None] * coarse[:, None, :, :], axis=2)

    def spread_with(modes, choice, weight_factors):
        scatter_copies = select_cluster(choice, weight_factors)
        return jnp.sum(modes[:, :, :, None] * scatter_copies[:, :, None, :], axis=1)

    def spread(weight_factors):
        return spread_with(rigid_body_modes, choice_matrix, weight_factors)

    def pair_sum(a, b):
        return jnp.sum(a * b, axis=(0, 1))

    def partner(entry_values, axis=1):
        half = entry_values.shape[axis] // 2
        lower = lax.slice_in_dim(entry_values, 0, half, axis=axis)
        upper = lax.slice_in_dim(entry_values, half, 2 * half, axis=axis)
        from_right = passed_along(upper, "sub", -1)
        from_left = passed_along(lower, "sub", 1)
        return jnp.concatenate([from_right, from_left], axis=axis)

    local_gram = jnp.einsum(
        "gmk,gnk->gmn", rigid_body_modes, rigid_body_modes, precision=HIGH_ACCURACY
    )
    gram_part = to_clusters(choice_matrix, local_gram)
    masked_modes = rigid_body_modes * jnp.swapaxes(free_mask, 1, 2)
    local_masked_gram = jnp.einsum(
        "gmk,gnk->gmn", masked_modes, rigid_body_modes, precision=HIGH_ACCURACY
    )
    masked_gram_part = to_clusters(choice_matrix, local_masked_gram)
    modes_count = rigid_body_modes.shape[1]
    site_data = jnp.concatenate(
        [
            rigid_body_modes,
            jnp.swapaxes(free_mask, 1, 2),
            jnp.broadcast_to(choice_matrix[:, :, None], (sub_count, clusters, row_count)),
        ],
        axis=1,
    )
    partner_data = partner(site_data, axis=2)
    partner_modes = partner_data[:, :modes_count]
    partner_free = jnp.swapaxes(partner_data[:, modes_count : modes_count + 1], 1, 2)
    partner_masked_modes = partner_modes * partner_data[:, modes_count : modes_count + 1]
    partner_choice = (
        partner_data[:, modes_count + 1 :, 0],
        partner_data[:, modes_count + 1 :, face_len],
    )

    def partner_spread(weight_factors):
        halves = []
        for half in range(2):
            rows = slice(half * face_len, (half + 1) * face_len)
            halves.append(spread_with(partner_modes[:, :, rows], partner_choice[half], weight_factors))
        return jnp.concatenate(halves, axis=1)

    def folded_coarse(signed_rows, own_modes, other_modes):
        own = partial_coarse_with(own_modes, choice_matrix, signed_rows)
        for half in range(2):
            rows = slice(half * face_len, (half + 1) * face_len)
            own = own + partial_coarse_with(
                other_modes[:, :, rows], partner_choice[half], signed_rows[:, rows]
            )
        return own

    masked_loads = row_major(free_mask * load_cases)
    partner_loads = partner(masked_loads)
    coarse_gram, masked_gram, coarse_first = total_over_devices(
        (gram_part, masked_gram_part, partial_coarse(masked_loads))
    )
    inverse = small_inverse(coarse_gram)

    first_weights = apply_blocks(inverse, coarse_first)
    residual = free_mask * (masked_loads - spread(first_weights))
    partner_res = partner_free * (partner_loads - partner_spread(first_weights))
    coarse_res = coarse_first - apply_blocks(masked_gram, first_weights)
    multipliers = jnp.zeros_like(load_cases)
    for iteration in range(ITERS):
        last = iteration + 1 == ITERS
        res_weights = apply_blocks(inverse, coarse_res)
        projected = residual - spread(res_weights)
        partner_proj = partner_res - partner_spread(res_weights)
        joined = face_sign * (projected + partner_proj)
        image_rows = jnp.einsum(
            "gkc,gcr->gkr",
            schur_blocks,
            lax.all_gather(joined, "face", axis=1, tiled=True),
            precision=HIGH_ACCURACY,
        )
        parts = [
            folded_coarse(face_sign * image_rows, rigid_body_modes, partner_modes),
            pair_sum(joined, image_rows),
            pair_sum(residual, residual),
        ]
        if iteration:
            parts.append(pair_sum(residual, image))
        if not last:
            parts.append(folded_coarse(face_sign * image_rows, masked_modes, partner_masked_modes))
        totals = total_over_devices(parts)
        signed = row_major(face_sign * image_rows)
        folded_now = signed + partner(signed)
        coarse_now, curvature_now, norm_next = totals[:3]
        masked_now = totals[-1] if not last else None
        if iteration:
            cross = totals[3]
            ratio = norm_next / norm_now
            direction = residual + ratio * direction
            curvature = curvature_now + 2.0 * ratio * cross + ratio * ratio * curvature
            coarse_out = coarse_now + ratio * coarse_out
            folded = folded_now + ratio * folded
            if not last:
                coarse_masked_out = masked_now + ratio * coarse_masked_out
        else:
            direction = residual
            curvature = curvature_now
            coarse_out = coarse_now
            folded = folded_now
            if not last:
                coarse_masked_out = masked_now
        norm_now = norm_next
        weights = apply_blocks(inverse, coarse_out)
        image = row_major(free_mask * (folded - spread(weights)))
        step_size = norm_now / curvature
        multipliers = row_major(multipliers + step_size * direction)
        residual = row_major(residual - step_size * image)
        if not last:
            partner_image = partner_free * (folded - partner_spread(weights))
            partner_res = partner_res - step_size * partner_image
            coarse_res = coarse_res - step_size * (
                coarse_masked_out - apply_blocks(masked_gram, weights)
            )
    return (multipliers, residual)


def solution(mesh):
    placed = (
        P("sub", "face", None),
        P("sub", None, "face"),
        P("sub", "face", None),
        P("sub", "face"),
        P("sub", "face"),
        P("sub", "face"),
        P("sub"),
        P("sub", "face", None, None),
    )
    return jax.shard_map(
        on_device,
        mesh=mesh,
        in_specs=placed,
        out_specs=(P("sub", "face", None), P("sub", "face", None)),
        check_vma=False,
    )
```

```python
import jax
import jax.numpy as jnp
from jax import lax
from jax.experimental.layout import Layout, with_layout_constraint
from jax.sharding import PartitionSpec as P

ITERS = 2
AXES = ("sub", "face")
ROUNDS = ((0,), (1, 2, 3), (4, 5), (6, 7))


HIGH_ACCURACY = lax.Precision.HIGHEST


def passed_along(value, axis, steps):
    count = lax.axis_size(axis)
    pairs = [(source, (source + steps) % count) for source in range(count)]
    return lax.ppermute(value, axis, pairs)


def row_major(value):
    return with_layout_constraint(value, Layout(major_to_minor=tuple(range(value.ndim))))


def total_over_devices(parts):
    count = lax.axis_size("sub") * lax.axis_size("face")
    flat = [jnp.ravel(part) for part in parts]
    sizes = [piece.shape[0] for piece in flat]
    packed = jnp.concatenate(flat)
    length = packed.shape[0]
    padded = -(-length // 2048) * 2048
    packed = jnp.pad(packed, (0, padded - length)).reshape(padded // 128, 128)
    if count & (count - 1) or count != 1 << 8 or lax.axis_size("face") != 2:
        packed = lax.psum(packed, AXES)
    else:
        half = padded // 256
        core = lax.axis_index("face")
        with jax.named_scope("round0"):
            kept = lax.dynamic_slice_in_dim(packed, core * half, half)
            given = lax.dynamic_slice_in_dim(packed, (1 - core) * half, half)
            kept = kept + lax.ppermute(given, AXES, [(source, source ^ 1) for source in range(count)])
        for number, field in enumerate(ROUNDS[1:], start=1):
            offsets = []
            for combo in range(1, 1 << len(field)):
                offsets.append(sum(1 << bit for i, bit in enumerate(field) if combo >> i & 1))
            with jax.named_scope(f"round{number}"):
                acc = kept
                for offset in offsets:
                    acc = acc + lax.ppermute(
                        kept, AXES, [(source, source ^ offset) for source in range(count)]
                    )
            kept = acc
        with jax.named_scope("gather"):
            other = lax.ppermute(kept, AXES, [(source, source ^ 1) for source in range(count)])
            packed = lax.dynamic_update_slice_in_dim(
                lax.dynamic_update_slice_in_dim(packed, kept, core * half, 0),
                other,
                (1 - core) * half,
                0,
            )
    packed = packed.reshape(padded)
    out = []
    start = 0
    for part, size in zip(parts, sizes):
        out.append(packed[start : start + size].reshape(part.shape))
        start += size
    return out


def small_inverse(gram):
    m = gram.shape[1]
    g = [[gram[:, i, j] for j in range(m)] for i in range(m)]
    low = [[None] * m for _ in range(m)]
    for j in range(m):
        acc = g[j][j]
        for k in range(j):
            acc = acc - low[j][k] * low[j][k]
        low[j][j] = jnp.sqrt(acc)
        for i in range(j + 1, m):
            acc = g[i][j]
            for k in range(j):
                acc = acc - low[i][k] * low[j][k]
            low[i][j] = acc / low[j][j]
    inv = [[None] * m for _ in range(m)]
    for c in range(m):
        for i in range(c, m):
            acc = jnp.ones_like(g[0][0]) if i == c else jnp.zeros_like(g[0][0])
            for k in range(c, i):
                acc = acc - low[i][k] * inv[k][c]
            inv[i][c] = acc / low[i][i]
    rows = []
    for a in range(m):
        row = []
        for b in range(m):
            acc = None
            for k in range(max(a, b), m):
                term = inv[k][a] * inv[k][b]
                acc = term if acc is None else acc + term
            row.append(acc)
        rows.append(jnp.stack(row, axis=-1))
    return jnp.stack(rows, axis=-2)


def on_device(
    schur_blocks,
    rigid_body_modes,
    load_cases,
    face_sizes,
    contact_mask,
    friction_mask,
    cluster_ids,
    pairing,
):
    sub_count, row_count, width = schur_blocks.shape
    columns = load_cases.shape[2]
    face_len = row_count // 2
    clusters = sub_count * lax.axis_size("sub") // 8
    positions = jnp.arange(face_len, dtype=jnp.int32)
    inside = (
        (positions[None, None, :] < face_sizes[:, :, None])
        .astype(jnp.float32)
        .reshape(sub_count, row_count)
    )
    blocked = (contact_mask * (1 - friction_mask)).astype(jnp.float32)
    free_mask = (inside * (1.0 - blocked))[:, :, None]
    choice_matrix = (cluster_ids[:, None] == jnp.arange(clusters, dtype=jnp.int32)[None, :]).astype(
        jnp.float32
    )
    face_sign = (1 - 2 * (jnp.arange(row_count, dtype=jnp.int32) // face_len)).astype(jnp.float32)[
        None, :, None
    ]

    def to_clusters(choice, part):
        return jnp.sum(choice[:, :, None, None] * part[:, None], axis=0)

    def select_cluster(choice, coarse):
        return jnp.sum(choice[:, :, None, None] * coarse[None], axis=1)

    def partial_coarse_with(modes, choice, entry_values):
        subdomain_part = jnp.einsum("hxy,hyj->hxj", modes, entry_values, precision=HIGH_ACCURACY)
        return to_clusters(choice, subdomain_part)

    def partial_coarse(entry_values):
        return partial_coarse_with(rigid_body_modes, choice_matrix, entry_values)

    def apply_blocks(blocks, coarse):
        return jnp.sum(blocks[:, :, :, None] * coarse[:, None, :, :], axis=2)

    def spread_with(modes, choice, weight_factors):
        scatter_copies = select_cluster(choice, weight_factors)
        return jnp.sum(modes[:, :, :, None] * scatter_copies[:, :, None, :], axis=1)

    def spread(weight_factors):
        return spread_with(rigid_body_modes, choice_matrix, weight_factors)

    def pair_sum(a, b):
        return jnp.sum(a * b, axis=(0, 1))

    def partner(entry_values, axis=1):
        half = entry_values.shape[axis] // 2
        lower = lax.slice_in_dim(entry_values, 0, half, axis=axis)
        upper = lax.slice_in_dim(entry_values, half, 2 * half, axis=axis)
        from_right = passed_along(upper, "sub", -1)
        from_left = passed_along(lower, "sub", 1)
        return jnp.concatenate([from_right, from_left], axis=axis)

    local_gram = jnp.einsum(
        "gmk,gnk->gmn", rigid_body_modes, rigid_body_modes, precision=HIGH_ACCURACY
    )
    gram_part = to_clusters(choice_matrix, local_gram)
    masked_modes = rigid_body_modes * jnp.swapaxes(free_mask, 1, 2)
    local_masked_gram = jnp.einsum(
        "gmk,gnk->gmn", masked_modes, rigid_body_modes, precision=HIGH_ACCURACY
    )
    masked_gram_part = to_clusters(choice_matrix, local_masked_gram)
    modes_count = rigid_body_modes.shape[1]
    site_data = jnp.concatenate(
        [
            rigid_body_modes,
            jnp.swapaxes(free_mask, 1, 2),
            jnp.broadcast_to(choice_matrix[:, :, None], (sub_count, clusters, row_count)),
        ],
        axis=1,
    )
    partner_data = partner(site_data, axis=2)
    partner_modes = partner_data[:, :modes_count]
    partner_free = jnp.swapaxes(partner_data[:, modes_count : modes_count + 1], 1, 2)
    partner_masked_modes = partner_modes * partner_data[:, modes_count : modes_count + 1]
    partner_choice = (
        partner_data[:, modes_count + 1 :, 0],
        partner_data[:, modes_count + 1 :, face_len],
    )

    def partner_spread(weight_factors):
        halves = []
        for half in range(2):
            rows = slice(half * face_len, (half + 1) * face_len)
            halves.append(spread_with(partner_modes[:, :, rows], partner_choice[half], weight_factors))
        return jnp.concatenate(halves, axis=1)

    def folded_coarse(signed_rows, own_modes, other_modes):
        own = partial_coarse_with(own_modes, choice_matrix, signed_rows)
        for half in range(2):
            rows = slice(half * face_len, (half + 1) * face_len)
            own = own + partial_coarse_with(
                other_modes[:, :, rows], partner_choice[half], signed_rows[:, rows]
            )
        return own

    masked_loads = row_major(free_mask * load_cases)
    partner_loads = partner(masked_loads)
    coarse_gram, masked_gram, coarse_first = total_over_devices(
        (gram_part, masked_gram_part, partial_coarse(masked_loads))
    )
    inverse = small_inverse(coarse_gram)

    first_weights = apply_blocks(inverse, coarse_first)
    residual = free_mask * (masked_loads - spread(first_weights))
    partner_res = partner_free * (partner_loads - partner_spread(first_weights))
    coarse_res = coarse_first - apply_blocks(masked_gram, first_weights)
    multipliers = jnp.zeros_like(load_cases)
    for iteration in range(ITERS):
        last = iteration + 1 == ITERS
        res_weights = apply_blocks(inverse, coarse_res)
        projected = residual - spread(res_weights)
        partner_proj = partner_res - partner_spread(res_weights)
        joined = face_sign * (projected + partner_proj)
        image_rows = jnp.einsum(
            "gkc,gcr->gkr",
            schur_blocks,
            lax.all_gather(joined, "face", axis=1, tiled=True),
            precision=HIGH_ACCURACY,
        )
        parts = [
            folded_coarse(face_sign * image_rows, rigid_body_modes, partner_modes),
            pair_sum(joined, image_rows),
            pair_sum(residual, residual),
        ]
        if iteration:
            parts.append(pair_sum(residual, image))
        if not last:
            parts.append(folded_coarse(face_sign * image_rows, masked_modes, partner_masked_modes))
        totals = total_over_devices(parts)
        signed = row_major(face_sign * image_rows)
        folded_now = signed + partner(signed)
        coarse_now, curvature_now, norm_next = totals[:3]
        masked_now = totals[-1] if not last else None
        if iteration:
            cross = totals[3]
            ratio = norm_next / norm_now
            direction = residual + ratio * direction
            curvature = curvature_now + 2.0 * ratio * cross + ratio * ratio * curvature
            coarse_out = coarse_now + ratio * coarse_out
            folded = folded_now + ratio * folded
            if not last:
                coarse_masked_out = masked_now + ratio * coarse_masked_out
        else:
            direction = residual
            curvature = curvature_now
            coarse_out = coarse_now
            folded = folded_now
            if not last:
                coarse_masked_out = masked_now
        norm_now = norm_next
        weights = apply_blocks(inverse, coarse_out)
        image = row_major(free_mask * (folded - spread(weights)))
        step_size = norm_now / curvature
        multipliers = row_major(multipliers + step_size * direction)
        residual = row_major(residual - step_size * image)
        if not last:
            partner_image = partner_free * (folded - partner_spread(weights))
            partner_res = partner_res - step_size * partner_image
            coarse_res = coarse_res - step_size * (
                coarse_masked_out - apply_blocks(masked_gram, weights)
            )
    return (multipliers, residual)


def solution(mesh):
    placed = (
        P("sub", "face", None),
        P("sub", None, "face"),
        P("sub", "face", None),
        P("sub", "face"),
        P("sub", "face"),
        P("sub", "face"),
        P("sub"),
        P("sub", "face", None, None),
    )
    return jax.shard_map(
        on_device,
        mesh=mesh,
        in_specs=placed,
        out_specs=(P("sub", "face", None), P("sub", "face", None)),
        check_vma=False,
    )
```
